32 devices in a mesh: grp: 2 (over x), gx: 16 (over z, y, core).
Axes of the slice: x: 2, y: 2, z: 4, core: 2. Of those that a mesh axis runs over, the one named last changes fastest.
Arguments:
- e_forward: float32 [3, 256, 32, 256], P(None, ('grp', 'gx')), parts along dimension 1, may hold values from -6 to 6
- h_forward: float32 [3, 256, 32, 256], P(None, ('grp', 'gx')), parts along dimension 1, may hold values from -6 to 6
- p_forward: float32 [3, 256, 32, 256], P(None, ('grp', 'gx')), parts along dimension 1, may hold values from -6 to 6
- j_forward: float32 [3, 256, 32, 256], P(None, ('grp', 'gx')), parts along dimension 1, may hold values from -6 to 6
- e_adjoint: float32 [3, 256, 32, 256], P(None, ('grp', 'gx')), parts along dimension 1, may hold values from -6 to 6
- h_adjoint: float32 [3, 256, 32, 256], P(None, ('grp', 'gx')), parts along dimension 1, may hold values from -6 to 6
- p_adjoint: float32 [3, 256, 32, 256], P(None, ('grp', 'gx')), parts along dimension 1, may hold values from -6 to 6
- j_adjoint: float32 [3, 256, 32, 256], P(None, ('grp', 'gx')), parts along dimension 1, may hold values from -6 to 6
- design: float32 [32, 32, 256], P(('grp', 'gx')), parts along dimension 0, may hold values from 0 to 1
- source_amp: float32 [32, 3], P('grp'), parts along dimension 0, may hold values from -6 to 6
- source_cell: int32 [32], P('grp'), parts along dimension 0, may hold values from 0 to 1048575
- monitor_cell: int32 [32], P('grp'), parts along dimension 0, may hold values from 0 to 1048575
- slab_start: int32 [2], P('grp'), parts along dimension 0, may hold values from 8 to 15
- radius: int32 [2], P('grp'), parts along dimension 0, may hold values from 1 to 4
Outputs:
- e_forward_next: float32 [3, 256, 32, 256], P(None, ('grp', 'gx')), parts along dimension 1
- h_forward_next: float32 [3, 256, 32, 256], P(None, ('grp', 'gx')), parts along dimension 1
- e_adjoint_next: float32 [3, 256, 32, 256], P(None, ('grp', 'gx')), parts along dimension 1
- h_adjoint_next: float32 [3, 256, 32, 256], P(None, ('grp', 'gx')), parts along dimension 1
- design_grad: float32 [32, 32, 256], P(('grp', 'gx')), parts along dimension 0
The draws below stay inside these ranges and needn't reach their ends.
There are 2 independent parts, one for each index of `grp`. The reference program is written for one: setup_inputs(seed, part) draws one part's arguments, and reference() takes and returns one part's arrays. A program takes and returns all parts, laid end to end along the dimension named above; each array names one. Nothing has to cross between parts.
Inputs may be any that keep to these rules, and one draw needn't show every extreme that they name: `slab_start`: the slab begins within planes 8 to 15 of the grid.
All inputs are finite; a program needn't handle non-finite values.
Results may differ from the reference program's by a relative error of at most 0.0003.
Values sent between devices are 32-bit elements; how exact they have to be, the bound alone decides.
No kernel may reach another device: no remote copies, remote signals or barrier semaphores. Data moves between devices by JAX's collectives and lax.ppermute only.
A program may use at most 128 MiB of HBM per device.

```python
import jax
import jax.numpy as jnp
from jax import lax

CZ = 8
NX = 32
NY = 256
NSRC = 16
NMON = 16
RMAX = 4
NZ = 128
DZ = 16


def set_ends(entries, stream_key, smallest, largest):
    place = [jax.random.randint(jax.random.fold_in(stream_key, axis), (), 0, length) for axis, length in enumerate(entries.shape)]
    widest = entries.shape.index(max(entries.shape))
    neighbour = place[:widest] + [(place[widest] + 1) % entries.shape[widest]] + place[widest + 1:]
    return entries.at[tuple(place)].set(smallest).at[tuple(neighbour)].set(largest)


def shard_levels(stream_key, shape, split, least, largest):
    def one(dim, shards_of):
        steps = jax.random.uniform(jax.random.fold_in(jax.random.fold_in(stream_key, 6), dim), (shards_of,), jnp.float32, least / len(split), largest / len(split))
        return jnp.repeat(jnp.exp(steps), shape[dim] // shards_of).reshape((-1,) + (1,) * (len(shape) - dim - 1))

    gain = one(*split[0])
    for cut in split[1:]:
        gain = gain * one(*cut)
    return gain


def gaussian(stream_key, dims, scale, reach, cuts=(), kind=jnp.bfloat16):
    entries = scale * jax.random.normal(stream_key, dims, jnp.float32)
    if cuts:
        entries = entries * shard_levels(stream_key, dims, cuts, -0.22, 0.18)
    return jnp.clip(entries, -reach, reach).astype(kind)


def setup_inputs(seed: int = 0, part: int = 0) -> dict:
    key_list = jax.random.split(jax.random.key(seed), 15)
    own_keys = jax.random.split(jax.random.fold_in(key_list[14], part), 15)
    e_forward = gaussian(own_keys[0], (3, NZ, NX, NY), 1.0, 6.0, ((1, 16),), jnp.float32)
    h_forward = gaussian(own_keys[1], (3, NZ, NX, NY), 1.0, 6.0, ((1, 16),), jnp.float32)
    p_forward = gaussian(own_keys[2], (3, NZ, NX, NY), 1.0, 6.0, ((1, 16),), jnp.float32)
    j_forward = gaussian(own_keys[3], (3, NZ, NX, NY), 1.0, 6.0, ((1, 16),), jnp.float32)
    e_adjoint = gaussian(own_keys[4], (3, NZ, NX, NY), 1.0, 6.0, ((1, 16),), jnp.float32)
    h_adjoint = gaussian(own_keys[5], (3, NZ, NX, NY), 1.0, 6.0, ((1, 16),), jnp.float32)
    p_adjoint = gaussian(own_keys[6], (3, NZ, NX, NY), 1.0, 6.0, ((1, 16),), jnp.float32)
    j_adjoint = gaussian(own_keys[7], (3, NZ, NX, NY), 1.0, 6.0, ((1, 16),), jnp.float32)
    design = jnp.clip(1.0 * jax.random.uniform(own_keys[8], (DZ, NX, NY), jnp.float32) ** shard_levels(own_keys[8], (DZ, NX, NY), ((0, 16),), -0.2, 0.2), 0.0, 1.0)
    source_amp = gaussian(own_keys[9], (NSRC, 3), 1.0, 6.0, (), jnp.float32)
    source_cell = set_ends(jax.random.randint(own_keys[10], (NSRC,), 0, NZ * NX * NY), jax.random.fold_in(own_keys[10], 1), 0, (NZ * NX * NY) - 1).astype(jnp.int32)
    monitor_cell = set_ends(jax.random.randint(own_keys[11], (NMON,), 0, NZ * NX * NY), jax.random.fold_in(own_keys[11], 1), 0, (NZ * NX * NY) - 1).astype(jnp.int32)
    slab_start = jax.random.randint(own_keys[12], (1,), CZ, 2 * CZ).astype(jnp.int32)
    radius = jax.random.randint(own_keys[13], (1,), 1, RMAX + 1).astype(jnp.int32)
    return dict(e_forward=e_forward, h_forward=h_forward, p_forward=p_forward, j_forward=j_forward, e_adjoint=e_adjoint, h_adjoint=h_adjoint, p_adjoint=p_adjoint, j_adjoint=j_adjoint, design=design, source_amp=source_amp, source_cell=source_cell, monitor_cell=monitor_cell, slab_start=slab_start, radius=radius)


DT = 0.5
EPS_RANGE = 10.0
STRENGTH_BASE = 0.5
STRENGTH_RANGE = 3.0
DAMPING = 0.2
GAIN_FIELD = 0.25
HIGH = lax.Precision.HIGHEST


def band_matrix(count, radius):
    rows = jnp.arange(count, dtype=jnp.int32)
    dist = jnp.abs(rows[:, None] - rows[None, :])
    weights = jnp.maximum(radius + 1 - dist, 0).astype(jnp.float32)
    return weights / jnp.sum(weights, axis=1, keepdims=True)


def ahead(field, axis):
    count = field.shape[axis]
    rest = lax.slice_in_dim(field, 1, count, axis=axis)
    return jnp.concatenate([rest, jnp.zeros_like(lax.slice_in_dim(field, 0, 1, axis=axis))], axis)


def behind(field, axis):
    count = field.shape[axis]
    rest = lax.slice_in_dim(field, 0, count - 1, axis=axis)
    return jnp.concatenate([jnp.zeros_like(lax.slice_in_dim(field, 0, 1, axis=axis)), rest], axis)


def update_h(efield, hfield):
    ex, ey, ez = efield[0], efield[1], efield[2]
    curl_x = (ahead(ez, 2) - ez) - (ahead(ey, 0) - ey)
    curl_y = (ahead(ex, 0) - ex) - (ahead(ez, 1) - ez)
    curl_z = (ahead(ey, 1) - ey) - (ahead(ex, 2) - ex)
    return hfield - DT * jnp.stack([curl_x, curl_y, curl_z])


def update_e(efield, hnext, jnext, permittivity, drive):
    hx, hy, hz = hnext[0], hnext[1], hnext[2]
    curl_x = (hz - behind(hz, 2)) - (hy - behind(hy, 0))
    curl_y = (hx - behind(hx, 0)) - (hz - behind(hz, 1))
    curl_z = (hy - behind(hy, 1)) - (hx - behind(hx, 2))
    curl = jnp.stack([curl_x, curl_y, curl_z])
    return efield + (DT / permittivity)[None] * (curl - jnext + drive)


def update_j(jfield, pfield, efield, strength):
    return ((1.0 - DAMPING * DT / 2.0) * jfield + DT * (strength[None] * efield - pfield)) / (1.0 + DAMPING * DT / 2.0)


def smooth(wx, wy, planes):
    inner = jnp.einsum("ax,zxy->zay", wx, planes, precision=HIGH)
    return jnp.einsum("zay,by->zab", inner, wy, precision=HIGH)


def smooth_adjoint(wx, wy, planes):
    inner = jnp.einsum("ax,zab->zxb", wx, planes, precision=HIGH)
    return jnp.einsum("zxb,by->zxy", inner, wy, precision=HIGH)


def split_cells(cells):
    zz = cells // (NX * NY)
    rest = cells % (NX * NY)
    return zz, rest // NY, rest % NY


def reference(e_forward, h_forward, p_forward, j_forward, e_adjoint, h_adjoint, p_adjoint, j_adjoint, design, source_amp, source_cell, monitor_cell, slab_start, radius):
    start = slab_start[0]
    wx = band_matrix(NX, radius[0])
    wy = band_matrix(NY, radius[0])
    rho_slab = smooth(wx, wy, design)
    zero = jnp.zeros((), jnp.int32)
    rho = lax.dynamic_update_slice(jnp.zeros((NZ, NX, NY), jnp.float32), rho_slab, (start, zero, zero))
    permittivity = 1.0 + EPS_RANGE * rho
    strength = STRENGTH_BASE + STRENGTH_RANGE * rho
    zs, xs, ys = split_cells(source_cell)
    drive = jnp.zeros((3, NZ, NX, NY), jnp.float32).at[:, zs, xs, ys].add(source_amp.T)
    zm, xm, ym = split_cells(monitor_cell)
    probe = e_forward[:, zm, xm, ym]
    drive_adj = jnp.zeros((3, NZ, NX, NY), jnp.float32).at[:, zm, xm, ym].add(probe)
    hf = update_h(e_forward, h_forward)
    ha = update_h(e_adjoint, h_adjoint)
    jf = update_j(j_forward, p_forward, e_forward, strength)
    ja = update_j(j_adjoint, p_adjoint, e_adjoint, strength)
    ef = update_e(e_forward, hf, jf, permittivity, drive)
    ea = update_e(e_adjoint, ha, ja, permittivity, drive_adj)
    intersection = jnp.sum(ea * ((ef - e_forward) + GAIN_FIELD * ef), axis=0)
    intersection_slab = lax.dynamic_slice(intersection, (start, zero, zero), (DZ, NX, NY))
    design_grad = smooth_adjoint(wx, wy, intersection_slab)
    return ef, hf, ea, ha, design_grad
```

```python
import jax
import jax.numpy as jnp
from jax import lax
from jax.sharding import PartitionSpec as P

DT = 0.5
EPS_RANGE = 10.0
STRENGTH_BASE = 0.5
STRENGTH_RANGE = 3.0
DAMPING = 0.2
GAIN_FIELD = 0.25
HIGH = lax.Precision.HIGHEST


def passed_along(block, axis, distance):
    devices = range(lax.axis_size(axis))
    route = [(i - distance, i) for i in devices if i - distance in devices]
    return lax.ppermute(block, axis, route)


def band_matrix(count, radius):
    rows = jnp.arange(count, dtype=jnp.int32)
    dist = jnp.abs(rows[:, None] - rows[None, :])
    weights = jnp.maximum(radius + 1 - dist, 0).astype(jnp.float32)
    return weights / jnp.sum(weights, axis=1, keepdims=True)


def ahead(field, axis):
    count = field.shape[axis]
    rest = lax.slice_in_dim(field, 1, count, axis=axis)
    return jnp.concatenate([rest, jnp.zeros_like(lax.slice_in_dim(field, 0, 1, axis=axis))], axis)


def behind(field, axis):
    count = field.shape[axis]
    rest = lax.slice_in_dim(field, 0, count - 1, axis=axis)
    return jnp.concatenate([jnp.zeros_like(lax.slice_in_dim(field, 0, 1, axis=axis)), rest], axis)


def update_h(efield, hfield, upper):
    ex, ey, ez = (efield[0], efield[1], efield[2])
    ex_next = jnp.concatenate([ex[1:], upper[0][None]], 0)
    ey_next = jnp.concatenate([ey[1:], upper[1][None]], 0)
    curl_x = ahead(ez, 2) - ez - (ey_next - ey)
    curl_y = ex_next - ex - (ahead(ez, 1) - ez)
    curl_z = ahead(ey, 1) - ey - (ahead(ex, 2) - ex)
    return hfield - DT * jnp.stack([curl_x, curl_y, curl_z])


def update_e(efield, hnext, lower, jnext, permittivity, drive):
    hx, hy, hz = (hnext[0], hnext[1], hnext[2])
    hx_prev = jnp.concatenate([lower[0][None], hx[:-1]], 0)
    hy_prev = jnp.concatenate([lower[1][None], hy[:-1]], 0)
    curl_x = hz - behind(hz, 2) - (hy - hy_prev)
    curl_y = hx - hx_prev - (hz - behind(hz, 1))
    curl_z = hy - behind(hy, 1) - (hx - behind(hx, 2))
    curl = jnp.stack([curl_x, curl_y, curl_z])
    return efield + (DT / permittivity)[None] * (curl - jnext + drive)


def update_j(jfield, pfield, efield, strength):
    return ((1.0 - DAMPING * DT / 2.0) * jfield + DT * (strength[None] * efield - pfield)) / (
        1.0 + DAMPING * DT / 2.0
    )


def smooth(wx, wy, planes):
    inner = jnp.einsum("ax,zxy->zay", wx, planes, precision=HIGH)
    return jnp.einsum("zay,by->zab", inner, wy, precision=HIGH)


def smooth_adjoint(wx, wy, planes):
    inner = jnp.einsum("ax,zab->zxb", wx, planes, precision=HIGH)
    return jnp.einsum("zxb,by->zxy", inner, wy, precision=HIGH)


def locate(cells, first, depth, width_x, width_y):
    zz = cells // (width_x * width_y)
    rest = cells % (width_x * width_y)
    local = zz - first
    inside = ((local >= 0) & (local < depth)).astype(jnp.float32)
    return (jnp.clip(local, 0, depth - 1), rest // width_y, rest % width_y, inside)


def body(
    e_forward,
    h_forward,
    p_forward,
    j_forward,
    e_adjoint,
    h_adjoint,
    p_adjoint,
    j_adjoint,
    design,
    source_amp,
    source_cell,
    monitor_cell,
    slab_start,
    radius,
):
    index = lax.axis_index("gx")
    depth, width_x, width_y = (e_forward.shape[1], e_forward.shape[2], e_forward.shape[3])
    start = slab_start[0]
    wx = band_matrix(width_x, radius[0])
    wy = band_matrix(width_y, radius[0])
    upper = passed_along(
        jnp.stack([e_forward[0, 0], e_forward[1, 0], e_adjoint[0, 0], e_adjoint[1, 0]]), "gx", -1
    )
    hf = update_h(e_forward, h_forward, upper[0:2])
    ha = update_h(e_adjoint, h_adjoint, upper[2:4])
    gathered = lax.all_gather(design, "gx", axis=0, tiled=True)
    slab = gathered.shape[0]
    planes = index * depth + jnp.arange(depth, dtype=jnp.int32) - start
    valid = ((planes >= 0) & (planes < slab)).astype(jnp.float32)
    picked = jnp.take(gathered, jnp.clip(planes, 0, slab - 1), axis=0) * valid[:, None, None]
    density = smooth(wx, wy, picked)
    permittivity = 1.0 + EPS_RANGE * density
    strength = STRENGTH_BASE + STRENGTH_RANGE * density
    lower = passed_along(jnp.stack([hf[0, -1], hf[1, -1], ha[0, -1], ha[1, -1]]), "gx", 1)
    zs, xs, ys, inside_s = locate(source_cell, index * depth, depth, width_x, width_y)
    nsrc = zs.shape[0]
    comp = jnp.repeat(jnp.arange(3, dtype=jnp.int32), nsrc)
    drive = (
        jnp.zeros((3, depth, width_x, width_y), jnp.float32)
        .at[comp, jnp.tile(zs, 3), jnp.tile(xs, 3), jnp.tile(ys, 3)]
        .add((source_amp.T * inside_s[None, :]).reshape(-1))
    )
    zm, xm, ym, inside_m = locate(monitor_cell, index * depth, depth, width_x, width_y)
    count = jnp.zeros((depth, width_x, width_y), jnp.float32).at[zm, xm, ym].add(inside_m)
    drive_adj = count[None] * e_forward
    jf = update_j(j_forward, p_forward, e_forward, strength)
    ja = update_j(j_adjoint, p_adjoint, e_adjoint, strength)
    ef = update_e(e_forward, hf, lower[0:2], jf, permittivity, drive)
    ea = update_e(e_adjoint, ha, lower[2:4], ja, permittivity, drive_adj)
    intersection = jnp.sum(ea * (ef - e_forward + GAIN_FIELD * ef), axis=0)
    slots = jnp.arange(slab, dtype=jnp.int32)
    select = (planes[:, None] == slots[None, :]).astype(jnp.float32)
    returned = jnp.einsum("lo,lxy->oxy", select, intersection, precision=HIGH)
    own_intersection = lax.psum_scatter(returned, "gx", scatter_dimension=0, tiled=True)
    design_grad = smooth_adjoint(wx, wy, own_intersection)
    return (ef, hf, ea, ha, design_grad)


def solution(mesh):
    return jax.shard_map(
        body,
        mesh=mesh,
        in_specs=(
            P(None, ("grp", "gx"), None, None),
            P(None, ("grp", "gx"), None, None),
            P(None, ("grp", "gx"), None, None),
            P(None, ("grp", "gx"), None, None),
            P(None, ("grp", "gx"), None, None),
            P(None, ("grp", "gx"), None, None),
            P(None, ("grp", "gx"), None, None),
            P(None, ("grp", "gx"), None, None),
            P(("grp", "gx"), None, None),
            P("grp", None),
            P("grp"),
            P("grp"),
            P("grp"),
            P("grp"),
        ),
        out_specs=(
            P(None, ("grp", "gx"), None, None),
            P(None, ("grp", "gx"), None, None),
            P(None, ("grp", "gx"), None, None),
            P(None, ("grp", "gx"), None, None),
            P(("grp", "gx"), None, None),
        ),
        check_vma=False,
    )
```

```python
import functools

import jax
import jax.numpy as jnp
from jax import lax
from jax.experimental import pallas as pl
from jax.experimental.pallas import tpu as pltpu
from jax.sharding import PartitionSpec as P

DT = 0.5
EPS_RANGE = 10.0
STRENGTH_BASE = 0.5
STRENGTH_RANGE = 3.0
DAMPING = 0.2
GAIN_FIELD = 0.25
HIGH = lax.Precision.HIGHEST
KEEP = 1.0 - DAMPING * DT / 2.0
LOSS = 1.0 + DAMPING * DT / 2.0


def passed_along(block, axis, distance):
    devices = range(lax.axis_size(axis))
    route = [(i - distance, i) for i in devices if i - distance in devices]
    return lax.ppermute(block, axis, route)


def band_matrix(count, radius):
    rows = jnp.arange(count, dtype=jnp.int32)
    dist = jnp.abs(rows[:, None] - rows[None, :])
    weights = jnp.maximum(radius + 1 - dist, 0).astype(jnp.float32)
    return weights / jnp.sum(weights, axis=1, keepdims=True)


def smooth(wx, wy, planes):
    inner = jnp.einsum("ax,zxy->zay", wx, planes, precision=HIGH)
    return jnp.einsum("zay,by->zab", inner, wy, precision=HIGH)


def smooth_adjoint(wx, wy, planes):
    inner = jnp.einsum("ax,zab->zxb", wx, planes, precision=HIGH)
    return jnp.einsum("zxb,by->zxy", inner, wy, precision=HIGH)


def field_kernel(
    ef, hf, pf, jf, ea, ha, pa, ja, rho, upper, below, src, mon, amp,
    ef_o, hf_o, ea_o, ha_o, inter_o,
):
    depth, width_x, width_y = rho.shape
    index = lax.axis_index("gx")
    row = lax.broadcasted_iota(jnp.int32, (width_x, width_y), 0)
    lane = lax.broadcasted_iota(jnp.int32, (width_x, width_y), 1)

    def ahead_y(f):
        return jnp.where(lane == width_y - 1, 0.0, pltpu.roll(f, width_y - 1, 1))

    def ahead_x(f):
        return jnp.where(row == width_x - 1, 0.0, pltpu.roll(f, width_x - 1, 0))

    def behind_y(f):
        return jnp.where(lane == 0, 0.0, pltpu.roll(f, 1, 1))

    def behind_x(f):
        return jnp.where(row == 0, 0.0, pltpu.roll(f, 1, 0))

    def new_h(e, h, z, ex_up, ey_up):
        ex, ey, ez = e[0, z], e[1, z], e[2, z]
        curl_x = ahead_y(ez) - ez - (ey_up - ey)
        curl_y = ex_up - ex - (ahead_x(ez) - ez)
        curl_z = ahead_x(ey) - ey - (ahead_y(ex) - ex)
        return (h[0, z] - DT * curl_x, h[1, z] - DT * curl_y, h[2, z] - DT * curl_z)

    def lower_h(e, base):
        hx, hy, ex, ey, ez = (below[base + i] for i in range(5))
        curl_x = ahead_y(ez) - ez - (e[1, 0] - ey)
        curl_y = e[0, 0] - ex - (ahead_x(ez) - ez)
        keep = index > 0
        return (
            jnp.where(keep, hx - DT * curl_x, 0.0),
            jnp.where(keep, hy - DT * curl_y, 0.0),
        )

    def new_e(e, p, j, out, z, hn, hn_dn, step, strength):
        hx, hy, hz = hn
        hx_dn, hy_dn = hn_dn
        curl = (
            hz - behind_y(hz) - (hy - hy_dn),
            hx - hx_dn - (hz - behind_x(hz)),
            hy - behind_x(hy) - (hx - behind_y(hx)),
        )
        for c in range(3):
            j_next = (KEEP * j[c, z] + DT * (strength * e[c, z] - p[c, z])) / LOSS
            out[c, z] = e[c, z] + step * (curl[c] - j_next)

    runs = ((ef, hf, pf, jf, hf_o, ef_o, 0), (ea, ha, pa, ja, ha_o, ea_o, 2))
    prev = [lower_h(ef, 0), lower_h(ea, 5)]
    for z in range(depth):
        density = rho[z]
        step = DT / (1.0 + EPS_RANGE * density)
        strength = STRENGTH_BASE + STRENGTH_RANGE * density
        for r, (e, h, p, j, h_out, e_out, up) in enumerate(runs):
            if z + 1 < depth:
                ex_up, ey_up = e[0, z + 1], e[1, z + 1]
            else:
                ex_up, ey_up = upper[up], upper[up + 1]
            hn = new_h(e, h, z, ex_up, ey_up)
            for c in range(3):
                h_out[c, z] = hn[c]
            new_e(e, p, j, e_out, z, hn, prev[r], step, strength)
            prev[r] = (hn[0], hn[1])

    plane = width_x * width_y
    tile_row = lax.broadcasted_iota(jnp.int32, (8, width_y), 0)
    tile_lane = lax.broadcasted_iota(jnp.int32, (8, width_y), 1)

    def add_at(cell, out, value_of):
        zz = cell // plane
        local = zz - index * depth
        rest = cell - zz * plane
        x = rest // width_y
        y = rest - x * width_y
        x0 = pl.multiple_of((x // 8) * 8, 8)

        @pl.when((local >= 0) & (local < depth))
        def _():
            rows = pl.ds(x0, 8)
            hit = (tile_row == x - x0) & (tile_lane == y)
            step = DT / (1.0 + EPS_RANGE * rho[local, rows, :])
            for c in range(3):
                held = out[c, local, rows, :]
                out[c, local, rows, :] = held + jnp.where(hit, step * value_of(c, local, rows), 0.0)

    for s in range(src.shape[0]):
        add_at(src[s], ef_o, lambda c, local, rows, s=s: amp[s, c])
    for m in range(mon.shape[0]):
        add_at(mon[m], ea_o, lambda c, local, rows: ef[c, local, rows, :])

    for z in range(depth):
        total = None
        for c in range(3):
            fwd = ef_o[c, z]
            term = ea_o[c, z] * (fwd - ef[c, z] + GAIN_FIELD * fwd)
            total = term if total is None else total + term
        inter_o[z] = total


def fields(e_forward, h_forward, p_forward, j_forward, e_adjoint, h_adjoint, p_adjoint, j_adjoint,
           density, upper, below, source_cell, monitor_cell, source_amp):
    shape = e_forward.shape
    depth = shape[1]
    field = jax.ShapeDtypeStruct(shape, jnp.float32)
    vmem = pl.BlockSpec(memory_space=pltpu.VMEM)
    smem = pl.BlockSpec(memory_space=pltpu.SMEM)
    cells = shape[1] * shape[2] * shape[3]
    return pl.pallas_call(
        field_kernel,
        out_shape=(field, field, field, field, jax.ShapeDtypeStruct(shape[1:], jnp.float32)),
        in_specs=[vmem] * 11 + [smem] * 3,
        out_specs=(vmem,) * 5,
        compiler_params=pltpu.CompilerParams(vmem_limit_bytes=48 * 1024 * 1024),
        cost_estimate=pl.CostEstimate(
            flops=200 * cells, bytes_accessed=4 * cells * 40, transcendentals=0
        ),
    )(e_forward, h_forward, p_forward, j_forward, e_adjoint, h_adjoint, p_adjoint, j_adjoint,
      density, upper, below, source_cell, monitor_cell, source_amp)


def body(
    e_forward,
    h_forward,
    p_forward,
    j_forward,
    e_adjoint,
    h_adjoint,
    p_adjoint,
    j_adjoint,
    design,
    source_amp,
    source_cell,
    monitor_cell,
    slab_start,
    radius,
):
    count = lax.axis_size("gx")
    index = lax.axis_index("gx")
    depth, width_x, width_y = (e_forward.shape[1], e_forward.shape[2], e_forward.shape[3])
    start = slab_start[0]
    wx = band_matrix(width_x, radius[0])
    wy = band_matrix(width_y, radius[0])
    planes = index * depth + jnp.arange(depth, dtype=jnp.int32) - start
    select = (planes[:, None] == jnp.arange(count, dtype=jnp.int32)[None, :]).astype(jnp.float32)
    upper = passed_along(
        jnp.stack([e_forward[0, 0], e_forward[1, 0], e_adjoint[0, 0], e_adjoint[1, 0]]), "gx", -1
    )
    below = passed_along(
        jnp.stack(
            [h_forward[0, -1], h_forward[1, -1], e_forward[0, -1], e_forward[1, -1], e_forward[2, -1],
             h_adjoint[0, -1], h_adjoint[1, -1], e_adjoint[0, -1], e_adjoint[1, -1], e_adjoint[2, -1]]
        ),
        "gx",
        1,
    )
    owned = smooth(wx, wy, design)
    holder = (start + index) // depth
    target = (jnp.arange(count, dtype=jnp.int32) == holder).astype(jnp.float32)
    slots = target[:, None, None] * owned
    arrived = lax.all_to_all(slots, "gx", split_axis=0, concat_axis=0, tiled=True)
    density = jnp.einsum("lo,oxy->lxy", select, arrived, precision=HIGH)
    ef, hf, ea, ha, intersection = fields(
        e_forward, h_forward, p_forward, j_forward, e_adjoint, h_adjoint, p_adjoint, j_adjoint,
        density, upper, below, source_cell, monitor_cell, source_amp,
    )
    returned = jnp.einsum("lo,lxy->oxy", select, intersection, precision=HIGH)
    arrived_back = lax.all_to_all(returned, "gx", split_axis=0, concat_axis=0, tiled=True)
    own_intersection = jnp.sum(arrived_back, axis=0, keepdims=True)
    design_grad = smooth_adjoint(wx, wy, own_intersection)
    return (ef, hf, ea, ha, design_grad)


def solution(mesh):
    return jax.shard_map(
        body,
        mesh=mesh,
        in_specs=(
            P(None, ("grp", "gx"), None, None),
            P(None, ("grp", "gx"), None, None),
            P(None, ("grp", "gx"), None, None),
            P(None, ("grp", "gx"), None, None),
            P(None, ("grp", "gx"), None, None),
            P(None, ("grp", "gx"), None, None),
            P(None, ("grp", "gx"), None, None),
            P(None, ("grp", "gx"), None, None),
            P(("grp", "gx"), None, None),
            P("grp", None),
            P("grp"),
            P("grp"),
            P("grp"),
            P("grp"),
        ),
        out_specs=(
            P(None, ("grp", "gx"), None, None),
            P(None, ("grp", "gx"), None, None),
            P(None, ("grp", "gx"), None, None),
            P(None, ("grp", "gx"), None, None),
            P(("grp", "gx"), None, None),
        ),
        check_vma=False,
    )
```

```python
import functools

import jax
import jax.numpy as jnp
from jax import lax
from jax.experimental import pallas as pl
from jax.experimental.pallas import tpu as pltpu
from jax.sharding import PartitionSpec as P

DT = 0.5
EPS_RANGE = 10.0
STRENGTH_BASE = 0.5
STRENGTH_RANGE = 3.0
DAMPING = 0.2
GAIN_FIELD = 0.25
HIGH = lax.Precision.HIGHEST
KEEP = 1.0 - DAMPING * DT / 2.0
LOSS = 1.0 + DAMPING * DT / 2.0


def passed_along(block, axis, distance):
    devices = range(lax.axis_size(axis))
    route = [(i - distance, i) for i in devices if i - distance in devices]
    return lax.ppermute(block, axis, route)


def band_matrix(count, radius):
    rows = jnp.arange(count, dtype=jnp.int32)
    dist = jnp.abs(rows[:, None] - rows[None, :])
    weights = jnp.maximum(radius + 1 - dist, 0).astype(jnp.float32)
    return weights / jnp.sum(weights, axis=1, keepdims=True)


def smooth(wx, wy, planes):
    inner = jnp.einsum("ax,zxy->zay", wx, planes, precision=HIGH)
    return jnp.einsum("zay,by->zab", inner, wy, precision=HIGH)


def smooth_adjoint(wx, wy, planes):
    inner = jnp.einsum("ax,zab->zxb", wx, planes, precision=HIGH)
    return jnp.einsum("zxb,by->zxy", inner, wy, precision=HIGH)


def field_kernel(
    ef, hf, pf, jf, ea, ha, pa, ja, arrived, upper, below, src, mon, amp, first,
    ef_o, hf_o, ea_o, ha_o, ret_o, rho,
):
    depth, width_x, width_y = rho.shape
    slab = arrived.shape[0]
    index = lax.axis_index("gx")
    start = first[0]
    for z in range(depth):
        p = index * depth + z - start
        inside = (p >= 0) & (p < slab)
        rho[z] = jnp.where(inside, arrived[jnp.clip(p, 0, slab - 1)], 0.0)
    row = lax.broadcasted_iota(jnp.int32, (width_x, width_y), 0)
    lane = lax.broadcasted_iota(jnp.int32, (width_x, width_y), 1)

    def ahead_y(f):
        return jnp.where(lane == width_y - 1, 0.0, pltpu.roll(f, width_y - 1, 1))

    def ahead_x(f):
        return jnp.where(row == width_x - 1, 0.0, pltpu.roll(f, width_x - 1, 0))

    def behind_y(f):
        return jnp.where(lane == 0, 0.0, pltpu.roll(f, 1, 1))

    def behind_x(f):
        return jnp.where(row == 0, 0.0, pltpu.roll(f, 1, 0))

    def new_h(e, h, z, ex_up, ey_up):
        ex, ey, ez = e[0, z], e[1, z], e[2, z]
        curl_x = ahead_y(ez) - ez - (ey_up - ey)
        curl_y = ex_up - ex - (ahead_x(ez) - ez)
        curl_z = ahead_x(ey) - ey - (ahead_y(ex) - ex)
        return (h[0, z] - DT * curl_x, h[1, z] - DT * curl_y, h[2, z] - DT * curl_z)

    def lower_h(e, base):
        hx, hy, ex, ey, ez = (below[base + i] for i in range(5))
        curl_x = ahead_y(ez) - ez - (e[1, 0] - ey)
        curl_y = e[0, 0] - ex - (ahead_x(ez) - ez)
        keep = index > 0
        return (
            jnp.where(keep, hx - DT * curl_x, 0.0),
            jnp.where(keep, hy - DT * curl_y, 0.0),
        )

    def new_e(e, p, j, out, z, hn, hn_dn, step, strength):
        hx, hy, hz = hn
        hx_dn, hy_dn = hn_dn
        curl = (
            hz - behind_y(hz) - (hy - hy_dn),
            hx - hx_dn - (hz - behind_x(hz)),
            hy - behind_x(hy) - (hx - behind_y(hx)),
        )
        for c in range(3):
            j_next = (KEEP * j[c, z] + DT * (strength * e[c, z] - p[c, z])) / LOSS
            out[c, z] = e[c, z] + step * (curl[c] - j_next)

    runs = ((ef, hf, pf, jf, hf_o, ef_o, 0), (ea, ha, pa, ja, ha_o, ea_o, 2))
    prev = [lower_h(ef, 0), lower_h(ea, 5)]
    for z in range(depth):
        density = rho[z]
        step = DT / (1.0 + EPS_RANGE * density)
        strength = STRENGTH_BASE + STRENGTH_RANGE * density
        for r, (e, h, p, j, h_out, e_out, up) in enumerate(runs):
            if z + 1 < depth:
                ex_up, ey_up = e[0, z + 1], e[1, z + 1]
            else:
                ex_up, ey_up = upper[up], upper[up + 1]
            hn = new_h(e, h, z, ex_up, ey_up)
            for c in range(3):
                h_out[c, z] = hn[c]
            new_e(e, p, j, e_out, z, hn, prev[r], step, strength)
            prev[r] = (hn[0], hn[1])

    plane = width_x * width_y
    tile_row = lax.broadcasted_iota(jnp.int32, (8, width_y), 0)
    tile_lane = lax.broadcasted_iota(jnp.int32, (8, width_y), 1)

    def add_at(cell, out, value_of):
        zz = cell // plane
        local = zz - index * depth
        rest = cell - zz * plane
        x = rest // width_y
        y = rest - x * width_y
        x0 = pl.multiple_of((x // 8) * 8, 8)

        @pl.when((local >= 0) & (local < depth))
        def _():
            rows = pl.ds(x0, 8)
            hit = (tile_row == x - x0) & (tile_lane == y)
            step = DT / (1.0 + EPS_RANGE * rho[local, rows, :])
            for c in range(3):
                held = out[c, local, rows, :]
                out[c, local, rows, :] = held + jnp.where(hit, step * value_of(c, local, rows), 0.0)

    for s in range(src.shape[0]):
        add_at(src[s], ef_o, lambda c, local, rows, s=s: amp[s, c])
    for m in range(mon.shape[0]):
        add_at(mon[m], ea_o, lambda c, local, rows: ef[c, local, rows, :])

    for g in range(slab):
        ret_o[g] = jnp.zeros((width_x, width_y), jnp.float32)
    for z in range(depth):
        total = None
        for c in range(3):
            fwd = ef_o[c, z]
            term = ea_o[c, z] * (fwd - ef[c, z] + GAIN_FIELD * fwd)
            total = term if total is None else total + term
        p = index * depth + z - start

        @pl.when((p >= 0) & (p < slab))
        def _():
            ret_o[jnp.clip(p, 0, slab - 1)] = total


def fields(e_forward, h_forward, p_forward, j_forward, e_adjoint, h_adjoint, p_adjoint, j_adjoint,
           arrived, upper, below, source_cell, monitor_cell, source_amp, slab_start):
    shape = e_forward.shape
    depth = shape[1]
    field = jax.ShapeDtypeStruct(shape, jnp.float32)
    vmem = pl.BlockSpec(memory_space=pltpu.VMEM)
    smem = pl.BlockSpec(memory_space=pltpu.SMEM)
    cells = shape[1] * shape[2] * shape[3]
    return pl.pallas_call(
        field_kernel,
        out_shape=(field, field, field, field, jax.ShapeDtypeStruct(arrived.shape, jnp.float32)),
        in_specs=[vmem] * 11 + [smem] * 4,
        out_specs=(vmem,) * 5,
        scratch_shapes=[pltpu.VMEM(shape[1:], jnp.float32)],
        compiler_params=pltpu.CompilerParams(vmem_limit_bytes=48 * 1024 * 1024),
        cost_estimate=pl.CostEstimate(
            flops=200 * cells, bytes_accessed=4 * cells * 40, transcendentals=0
        ),
    )(e_forward, h_forward, p_forward, j_forward, e_adjoint, h_adjoint, p_adjoint, j_adjoint,
      arrived, upper, below, source_cell, monitor_cell, source_amp, slab_start)


def body(
    e_forward,
    h_forward,
    p_forward,
    j_forward,
    e_adjoint,
    h_adjoint,
    p_adjoint,
    j_adjoint,
    design,
    source_amp,
    source_cell,
    monitor_cell,
    slab_start,
    radius,
):
    count = lax.axis_size("gx")
    index = lax.axis_index("gx")
    depth, width_x, width_y = (e_forward.shape[1], e_forward.shape[2], e_forward.shape[3])
    start = slab_start[0]
    wx = band_matrix(width_x, radius[0])
    wy = band_matrix(width_y, radius[0])
    upper = passed_along(jnp.concatenate([e_forward[0:2, 0], e_adjoint[0:2, 0]], 0), "gx", -1)
    below = passed_along(
        jnp.concatenate(
            [h_forward[0:2, -1], e_forward[:, -1], h_adjoint[0:2, -1], e_adjoint[:, -1]], 0
        ),
        "gx",
        1,
    )
    owned = smooth(wx, wy, design)
    holder = (start + index) // depth
    target = (jnp.arange(count, dtype=jnp.int32) == holder).astype(jnp.float32)
    slots = target[:, None, None] * owned
    arrived = lax.all_to_all(slots, "gx", split_axis=0, concat_axis=0, tiled=True)
    ef, hf, ea, ha, returned = fields(
        e_forward, h_forward, p_forward, j_forward, e_adjoint, h_adjoint, p_adjoint, j_adjoint,
        arrived, upper, below, source_cell, monitor_cell, source_amp, slab_start,
    )
    arrived_back = lax.all_to_all(returned, "gx", split_axis=0, concat_axis=0, tiled=True)
    inner = jnp.einsum("ax,jab->xb", wx, arrived_back, precision=HIGH)
    design_grad = jnp.einsum("xb,by->xy", inner, wy, precision=HIGH)[None]
    return (ef, hf, ea, ha, design_grad)


def solution(mesh):
    return jax.shard_map(
        body,
        mesh=mesh,
        in_specs=(
            P(None, ("grp", "gx"), None, None),
            P(None, ("grp", "gx"), None, None),
            P(None, ("grp", "gx"), None, None),
            P(None, ("grp", "gx"), None, None),
            P(None, ("grp", "gx"), None, None),
            P(None, ("grp", "gx"), None, None),
            P(None, ("grp", "gx"), None, None),
            P(None, ("grp", "gx"), None, None),
            P(("grp", "gx"), None, None),
            P("grp", None),
            P("grp"),
            P("grp"),
            P("grp"),
            P("grp"),
        ),
        out_specs=(
            P(None, ("grp", "gx"), None, None),
            P(None, ("grp", "gx"), None, None),
            P(None, ("grp", "gx"), None, None),
            P(None, ("grp", "gx"), None, None),
            P(("grp", "gx"), None, None),
        ),
        check_vma=False,
    )
```

```python
import functools

import jax
import jax.numpy as jnp
from jax import lax
from jax.experimental import pallas as pl
from jax.experimental.pallas import tpu as pltpu
from jax.sharding import PartitionSpec as P

DT = 0.5
EPS_RANGE = 10.0
STRENGTH_BASE = 0.5
STRENGTH_RANGE = 3.0
DAMPING = 0.2
GAIN_FIELD = 0.25
HIGH = lax.Precision.HIGHEST
KEEP = 1.0 - DAMPING * DT / 2.0
LOSS = 1.0 + DAMPING * DT / 2.0


def passed_along(block, axis, distance):
    devices = range(lax.axis_size(axis))
    route = [(i - distance, i) for i in devices if i - distance in devices]
    return lax.ppermute(block, axis, route)


def band_matrix(count, radius):
    rows = jnp.arange(count, dtype=jnp.int32)
    dist = jnp.abs(rows[:, None] - rows[None, :])
    weights = jnp.maximum(radius + 1 - dist, 0).astype(jnp.float32)
    return weights / jnp.sum(weights, axis=1, keepdims=True)


def smooth(wx, wy, planes):
    inner = jnp.einsum("ax,zxy->zay", wx, planes, precision=HIGH)
    return jnp.einsum("zay,by->zab", inner, wy, precision=HIGH)


def smooth_adjoint(wx, wy, planes):
    inner = jnp.einsum("ax,zab->zxb", wx, planes, precision=HIGH)
    return jnp.einsum("zxb,by->zxy", inner, wy, precision=HIGH)


def field_kernel(
    ef, hf, pf, jf, ea, ha, pa, ja, ef_up, ea_up, arrived, upper, below, src, mon, amp, first,
    ef_o, hf_o, ea_o, ha_o, ret_o, prev, rho,
):
    _, _, width_x, width_y = ef.shape
    depth = pl.num_programs(0)
    z = pl.program_id(0)
    slab = arrived.shape[0]
    index = lax.axis_index("gx")
    start = first[0]
    row = lax.broadcasted_iota(jnp.int32, (width_x, width_y), 0)
    lane = lax.broadcasted_iota(jnp.int32, (width_x, width_y), 1)

    def ahead_y(f):
        return jnp.where(lane == width_y - 1, 0.0, pltpu.roll(f, width_y - 1, 1))

    def ahead_x(f):
        return jnp.where(row == width_x - 1, 0.0, pltpu.roll(f, width_x - 1, 0))

    def behind_y(f):
        return jnp.where(lane == 0, 0.0, pltpu.roll(f, 1, 1))

    def behind_x(f):
        return jnp.where(row == 0, 0.0, pltpu.roll(f, 1, 0))

    p_here = index * depth + z - start
    inside = (p_here >= 0) & (p_here < slab)
    density = jnp.where(inside, arrived[jnp.clip(p_here, 0, slab - 1)], 0.0)
    rho[...] = density
    step = DT / (1.0 + EPS_RANGE * density)
    strength = STRENGTH_BASE + STRENGTH_RANGE * density
    last = z == depth - 1

    @pl.when(z == 0)
    def _():
        keep = index > 0
        for r, e in enumerate((ef, ea)):
            hx, hy, ex, ey, ez = (below[5 * r + i] for i in range(5))
            curl_x = ahead_y(ez) - ez - (e[1, 0] - ey)
            curl_y = e[0, 0] - ex - (ahead_x(ez) - ez)
            prev[2 * r] = jnp.where(keep, hx - DT * curl_x, 0.0)
            prev[2 * r + 1] = jnp.where(keep, hy - DT * curl_y, 0.0)
        for g in range(slab):
            ret_o[g] = jnp.zeros((width_x, width_y), jnp.float32)

    runs = ((ef, hf, pf, jf, ef_up, hf_o, ef_o), (ea, ha, pa, ja, ea_up, ha_o, ea_o))
    for r, (e, h, p, j, e_up, h_out, e_out) in enumerate(runs):
        ex, ey, ez = e[0, 0], e[1, 0], e[2, 0]
        ex_up = jnp.where(last, upper[2 * r], e_up[0, 0])
        ey_up = jnp.where(last, upper[2 * r + 1], e_up[1, 0])
        hx = h[0, 0] - DT * (ahead_y(ez) - ez - (ey_up - ey))
        hy = h[1, 0] - DT * (ex_up - ex - (ahead_x(ez) - ez))
        hz = h[2, 0] - DT * (ahead_x(ey) - ey - (ahead_y(ex) - ex))
        h_out[0, 0] = hx
        h_out[1, 0] = hy
        h_out[2, 0] = hz
        hx_dn = prev[2 * r]
        hy_dn = prev[2 * r + 1]
        curl = (
            hz - behind_y(hz) - (hy - hy_dn),
            hx - hx_dn - (hz - behind_x(hz)),
            hy - behind_x(hy) - (hx - behind_y(hx)),
        )
        for c in range(3):
            j_next = (KEEP * j[c, 0] + DT * (strength * e[c, 0] - p[c, 0])) / LOSS
            e_out[c, 0] = e[c, 0] + step * (curl[c] - j_next)
        prev[2 * r] = hx
        prev[2 * r + 1] = hy

    plane = width_x * width_y
    tile_row = lax.broadcasted_iota(jnp.int32, (8, width_y), 0)
    tile_lane = lax.broadcasted_iota(jnp.int32, (8, width_y), 1)

    def add_at(cell, out, value_of):
        zz = cell // plane
        rest = cell - zz * plane
        x = rest // width_y
        y = rest - x * width_y
        x0 = pl.multiple_of((x // 8) * 8, 8)

        @pl.when(zz - index * depth == z)
        def _():
            rows = pl.ds(x0, 8)
            hit = (tile_row == x - x0) & (tile_lane == y)
            gain = DT / (1.0 + EPS_RANGE * rho[rows, :])
            for c in range(3):
                held = out[c, 0, rows, :]
                out[c, 0, rows, :] = held + jnp.where(hit, gain * value_of(c, rows), 0.0)

    for s_ in range(src.shape[0]):
        add_at(src[s_], ef_o, lambda c, rows, s_=s_: amp[s_, c])
    for m in range(mon.shape[0]):
        add_at(mon[m], ea_o, lambda c, rows: ef[c, 0, rows, :])

    total = None
    for c in range(3):
        fwd = ef_o[c, 0]
        term = ea_o[c, 0] * (fwd - ef[c, 0] + GAIN_FIELD * fwd)
        total = term if total is None else total + term

    @pl.when(inside)
    def _():
        ret_o[jnp.clip(p_here, 0, slab - 1)] = total


def fields(e_forward, h_forward, p_forward, j_forward, e_adjoint, h_adjoint, p_adjoint, j_adjoint,
           arrived, upper, below, source_cell, monitor_cell, source_amp, slab_start):
    shape = e_forward.shape
    depth, width_x, width_y = shape[1], shape[2], shape[3]
    field = jax.ShapeDtypeStruct(shape, jnp.float32)
    block = pl.BlockSpec((3, 1, width_x, width_y), lambda z: (0, z, 0, 0))
    ahead = pl.BlockSpec((2, 1, width_x, width_y), lambda z: (0, jnp.minimum(z + 1, depth - 1), 0, 0))
    whole = lambda a: pl.BlockSpec(a.shape, lambda z: (0,) * a.ndim)
    smem = pl.BlockSpec(memory_space=pltpu.SMEM)
    cells = depth * width_x * width_y
    return pl.pallas_call(
        field_kernel,
        grid=(depth,),
        out_shape=(field, field, field, field, jax.ShapeDtypeStruct(arrived.shape, jnp.float32)),
        in_specs=[block] * 8 + [ahead] * 2 + [whole(arrived), whole(upper), whole(below)] + [smem] * 4,
        out_specs=(block,) * 4 + (whole(arrived),),
        scratch_shapes=[
            pltpu.VMEM((4, width_x, width_y), jnp.float32),
            pltpu.VMEM((width_x, width_y), jnp.float32),
        ],
        compiler_params=pltpu.CompilerParams(dimension_semantics=("arbitrary",)),
        cost_estimate=pl.CostEstimate(
            flops=200 * cells, bytes_accessed=4 * cells * 40, transcendentals=0
        ),
    )(e_forward, h_forward, p_forward, j_forward, e_adjoint, h_adjoint, p_adjoint, j_adjoint,
      e_forward, e_adjoint, arrived, upper, below, source_cell, monitor_cell, source_amp, slab_start)


def body(
    e_forward,
    h_forward,
    p_forward,
    j_forward,
    e_adjoint,
    h_adjoint,
    p_adjoint,
    j_adjoint,
    design,
    source_amp,
    source_cell,
    monitor_cell,
    slab_start,
    radius,
):
    count = lax.axis_size("gx")
    index = lax.axis_index("gx")
    depth, width_x, width_y = (e_forward.shape[1], e_forward.shape[2], e_forward.shape[3])
    start = slab_start[0]
    wx = band_matrix(width_x, radius[0])
    wy = band_matrix(width_y, radius[0])
    upper = passed_along(jnp.concatenate([e_forward[0:2, 0], e_adjoint[0:2, 0]], 0), "gx", -1)
    below = passed_along(
        jnp.concatenate(
            [h_forward[0:2, -1], e_forward[:, -1], h_adjoint[0:2, -1], e_adjoint[:, -1]], 0
        ),
        "gx",
        1,
    )
    owned = smooth(wx, wy, design)
    holder = (start + index) // depth
    target = (jnp.arange(count, dtype=jnp.int32) == holder).astype(jnp.float32)
    slots = target[:, None, None] * owned
    arrived = lax.all_to_all(slots, "gx", split_axis=0, concat_axis=0, tiled=True)
    ef, hf, ea, ha, returned = fields(
        e_forward, h_forward, p_forward, j_forward, e_adjoint, h_adjoint, p_adjoint, j_adjoint,
        arrived, upper, below, source_cell, monitor_cell, source_amp, slab_start,
    )
    arrived_back = lax.all_to_all(returned, "gx", split_axis=0, concat_axis=0, tiled=True)
    inner = jnp.einsum("ax,jab->xb", wx, arrived_back, precision=HIGH)
    design_grad = jnp.einsum("xb,by->xy", inner, wy, precision=HIGH)[None]
    return (ef, hf, ea, ha, design_grad)


def solution(mesh):
    return jax.shard_map(
        body,
        mesh=mesh,
        in_specs=(
            P(None, ("grp", "gx"), None, None),
            P(None, ("grp", "gx"), None, None),
            P(None, ("grp", "gx"), None, None),
            P(None, ("grp", "gx"), None, None),
            P(None, ("grp", "gx"), None, None),
            P(None, ("grp", "gx"), None, None),
            P(None, ("grp", "gx"), None, None),
            P(None, ("grp", "gx"), None, None),
            P(("grp", "gx"), None, None),
            P("grp", None),
            P("grp"),
            P("grp"),
            P("grp"),
            P("grp"),
        ),
        out_specs=(
            P(None, ("grp", "gx"), None, None),
            P(None, ("grp", "gx"), None, None),
            P(None, ("grp", "gx"), None, None),
            P(None, ("grp", "gx"), None, None),
            P(("grp", "gx"), None, None),
        ),
        check_vma=False,
    )
```

```python
import functools

import jax
import jax.numpy as jnp
from jax import lax
from jax.experimental import pallas as pl
from jax.experimental.pallas import tpu as pltpu
from jax.sharding import PartitionSpec as P

DT = 0.5
EPS_RANGE = 10.0
STRENGTH_BASE = 0.5
STRENGTH_RANGE = 3.0
DAMPING = 0.2
GAIN_FIELD = 0.25
HIGH = lax.Precision.HIGHEST
KEEP = 1.0 - DAMPING * DT / 2.0
LOSS = 1.0 + DAMPING * DT / 2.0


def passed_along(block, axis, distance):
    devices = range(lax.axis_size(axis))
    route = [(i - distance, i) for i in devices if i - distance in devices]
    return lax.ppermute(block, axis, route)


def band_matrix(count, radius):
    rows = jnp.arange(count, dtype=jnp.int32)
    dist = jnp.abs(rows[:, None] - rows[None, :])
    weights = jnp.maximum(radius + 1 - dist, 0).astype(jnp.float32)
    return weights / jnp.sum(weights, axis=1, keepdims=True)


def smooth(wx, wy, planes):
    inner = jnp.einsum("ax,zxy->zay", wx, planes, precision=HIGH)
    return jnp.einsum("zay,by->zab", inner, wy, precision=HIGH)


def smooth_adjoint(wx, wy, planes):
    inner = jnp.einsum("ax,zab->zxb", wx, planes, precision=HIGH)
    return jnp.einsum("zxb,by->zxy", inner, wy, precision=HIGH)


def field_kernel(
    ef_h, hf_h, pf_h, jf_h, ea_h, ha_h, pa_h, ja_h, arrived, upper, below, src, mon, amp, first,
    ef_oh, hf_oh, ea_oh, ha_oh, ret_o,
    ins, outs, rho, in_sem, out_sem,
):
    depth, width_x, width_y = rho.shape
    slab = arrived.shape[0]
    index = lax.axis_index("gx")
    start = first[0]
    sources = (ef_h, hf_h, pf_h, jf_h, ea_h, ha_h, pa_h, ja_h)
    targets = (ef_oh, hf_oh, ea_oh, ha_oh)

    def fetch(a, z):
        return pltpu.make_async_copy(
            sources[a].at[:, pl.ds(z, 1)], ins.at[a, :, pl.ds(z, 1)], in_sem.at[a, z]
        )

    def store(a, z):
        return pltpu.make_async_copy(
            outs.at[a, :, pl.ds(z, 1)], targets[a].at[:, pl.ds(z, 1)], out_sem.at[a, z]
        )

    for z in range(depth):
        for a in range(8):
            fetch(a, z).start()

    for z in range(depth):
        p = index * depth + z - start
        inside = (p >= 0) & (p < slab)
        rho[z] = jnp.where(inside, arrived[jnp.clip(p, 0, slab - 1)], 0.0)
    for g in range(slab):
        ret_o[g] = jnp.zeros((width_x, width_y), jnp.float32)

    row = lax.broadcasted_iota(jnp.int32, (width_x, width_y), 0)
    lane = lax.broadcasted_iota(jnp.int32, (width_x, width_y), 1)

    def ahead_y(f):
        return jnp.where(lane == width_y - 1, 0.0, pltpu.roll(f, width_y - 1, 1))

    def ahead_x(f):
        return jnp.where(row == width_x - 1, 0.0, pltpu.roll(f, width_x - 1, 0))

    def behind_y(f):
        return jnp.where(lane == 0, 0.0, pltpu.roll(f, 1, 1))

    def behind_x(f):
        return jnp.where(row == 0, 0.0, pltpu.roll(f, 1, 0))

    plane = width_x * width_y
    tile_row = lax.broadcasted_iota(jnp.int32, (8, width_y), 0)
    tile_lane = lax.broadcasted_iota(jnp.int32, (8, width_y), 1)

    def locate(cell):
        zz = cell // plane
        rest = cell - zz * plane
        x = rest // width_y
        y = rest - x * width_y
        return zz - index * depth, x, y

    src_at = [locate(src[s]) for s in range(src.shape[0])]
    mon_at = [locate(mon[m]) for m in range(mon.shape[0])]

    def add_at(where_, z, out, value_of):
        local, x, y = where_
        x0 = pl.multiple_of((x // 8) * 8, 8)

        @pl.when(local == z)
        def _():
            rows = pl.ds(x0, 8)
            hit = (tile_row == x - x0) & (tile_lane == y)
            gain = DT / (1.0 + EPS_RANGE * rho[z, rows, :])
            for c in range(3):
                held = outs[out, c, z, rows, :]
                outs[out, c, z, rows, :] = held + jnp.where(hit, gain * value_of(c, z, rows), 0.0)

    keep = index > 0
    prev = []
    for r in range(2):
        fetch(4 * r, 0).wait()
        fetch(4 * r + 1, 0).wait()
        hx, hy, ex, ey, ez = (below[5 * r + i] for i in range(5))
        e = ins.at[4 * r]
        curl_x = ahead_y(ez) - ez - (e[1, 0] - ey)
        curl_y = e[0, 0] - ex - (ahead_x(ez) - ez)
        prev.append((jnp.where(keep, hx - DT * curl_x, 0.0), jnp.where(keep, hy - DT * curl_y, 0.0)))
    for r in range(2):
        fetch(4 * r + 2, 0).wait()
        fetch(4 * r + 3, 0).wait()

    for z in range(depth):
        if z + 1 < depth:
            for a in range(8):
                fetch(a, z + 1).wait()
        density = rho[z]
        step = DT / (1.0 + EPS_RANGE * density)
        strength = STRENGTH_BASE + STRENGTH_RANGE * density
        for r in range(2):
            e, h, p, j = (ins.at[4 * r + i] for i in range(4))
            if z + 1 < depth:
                ex_up, ey_up = e[0, z + 1], e[1, z + 1]
            else:
                ex_up, ey_up = upper[2 * r], upper[2 * r + 1]
            ex, ey, ez = e[0, z], e[1, z], e[2, z]
            hx = h[0, z] - DT * (ahead_y(ez) - ez - (ey_up - ey))
            hy = h[1, z] - DT * (ex_up - ex - (ahead_x(ez) - ez))
            hz = h[2, z] - DT * (ahead_x(ey) - ey - (ahead_y(ex) - ex))
            outs[2 * r + 1, 0, z] = hx
            outs[2 * r + 1, 1, z] = hy
            outs[2 * r + 1, 2, z] = hz
            hx_dn, hy_dn = prev[r]
            curl = (
                hz - behind_y(hz) - (hy - hy_dn),
                hx - hx_dn - (hz - behind_x(hz)),
                hy - behind_x(hy) - (hx - behind_y(hx)),
            )
            for c in range(3):
                j_next = (KEEP * j[c, z] + DT * (strength * e[c, z] - p[c, z])) / LOSS
                outs[2 * r, c, z] = e[c, z] + step * (curl[c] - j_next)
            prev[r] = (hx, hy)
            store(2 * r + 1, z).start()

        for s in range(src.shape[0]):
            add_at(src_at[s], z, 0, lambda c, zz, rows, s=s: amp[s, c])
        for m in range(mon.shape[0]):
            add_at(mon_at[m], z, 2, lambda c, zz, rows: ins[0, c, zz, rows, :])
        store(0, z).start()
        store(2, z).start()

        total = None
        for c in range(3):
            fwd = outs[0, c, z]
            term = outs[2, c, z] * (fwd - ins[0, c, z] + GAIN_FIELD * fwd)
            total = term if total is None else total + term
        p = index * depth + z - start

        @pl.when((p >= 0) & (p < slab))
        def _():
            ret_o[jnp.clip(p, 0, slab - 1)] = total

    for z in range(depth):
        for a in range(4):
            store(a, z).wait()


def fields(e_forward, h_forward, p_forward, j_forward, e_adjoint, h_adjoint, p_adjoint, j_adjoint,
           arrived, upper, below, source_cell, monitor_cell, source_amp, slab_start):
    shape = e_forward.shape
    depth = shape[1]
    field = jax.ShapeDtypeStruct(shape, jnp.float32)
    hbm = pl.BlockSpec(memory_space=pltpu.HBM)
    vmem = pl.BlockSpec(memory_space=pltpu.VMEM)
    smem = pl.BlockSpec(memory_space=pltpu.SMEM)
    cells = shape[1] * shape[2] * shape[3]
    return pl.pallas_call(
        field_kernel,
        out_shape=(field, field, field, field, jax.ShapeDtypeStruct(arrived.shape, jnp.float32)),
        in_specs=[hbm] * 8 + [vmem] * 3 + [smem] * 4,
        out_specs=(hbm,) * 4 + (vmem,),
        scratch_shapes=[
            pltpu.VMEM((8,) + shape, jnp.float32),
            pltpu.VMEM((4,) + shape, jnp.float32),
            pltpu.VMEM(shape[1:], jnp.float32),
            pltpu.SemaphoreType.DMA((8, depth)),
            pltpu.SemaphoreType.DMA((4, depth)),
        ],
        compiler_params=pltpu.CompilerParams(vmem_limit_bytes=48 * 1024 * 1024),
        cost_estimate=pl.CostEstimate(
            flops=200 * cells, bytes_accessed=4 * cells * 40, transcendentals=0
        ),
    )(e_forward, h_forward, p_forward, j_forward, e_adjoint, h_adjoint, p_adjoint, j_adjoint,
      arrived, upper, below, source_cell, monitor_cell, source_amp, slab_start)


def body(
    e_forward,
    h_forward,
    p_forward,
    j_forward,
    e_adjoint,
    h_adjoint,
    p_adjoint,
    j_adjoint,
    design,
    source_amp,
    source_cell,
    monitor_cell,
    slab_start,
    radius,
):
    count = lax.axis_size("gx")
    index = lax.axis_index("gx")
    depth, width_x, width_y = (e_forward.shape[1], e_forward.shape[2], e_forward.shape[3])
    start = slab_start[0]
    wx = band_matrix(width_x, radius[0])
    wy = band_matrix(width_y, radius[0])
    upper = passed_along(jnp.concatenate([e_forward[0:2, 0], e_adjoint[0:2, 0]], 0), "gx", -1)
    below = passed_along(
        jnp.concatenate(
            [h_forward[0:2, -1], e_forward[:, -1], h_adjoint[0:2, -1], e_adjoint[:, -1]], 0
        ),
        "gx",
        1,
    )
    owned = smooth(wx, wy, design)
    holder = (start + index) // depth
    target = (jnp.arange(count, dtype=jnp.int32) == holder).astype(jnp.float32)
    slots = target[:, None, None] * owned
    arrived = lax.all_to_all(slots, "gx", split_axis=0, concat_axis=0, tiled=True)
    ef, hf, ea, ha, returned = fields(
        e_forward, h_forward, p_forward, j_forward, e_adjoint, h_adjoint, p_adjoint, j_adjoint,
        arrived, upper, below, source_cell, monitor_cell, source_amp, slab_start,
    )
    arrived_back = lax.all_to_all(returned, "gx", split_axis=0, concat_axis=0, tiled=True)
    inner = jnp.einsum("ax,jab->xb", wx, arrived_back, precision=HIGH)
    design_grad = jnp.einsum("xb,by->xy", inner, wy, precision=HIGH)[None]
    return (ef, hf, ea, ha, design_grad)


def solution(mesh):
    return jax.shard_map(
        body,
        mesh=mesh,
        in_specs=(
            P(None, ("grp", "gx"), None, None),
            P(None, ("grp", "gx"), None, None),
            P(None, ("grp", "gx"), None, None),
            P(None, ("grp", "gx"), None, None),
            P(None, ("grp", "gx"), None, None),
            P(None, ("grp", "gx"), None, None),
            P(None, ("grp", "gx"), None, None),
            P(None, ("grp", "gx"), None, None),
            P(("grp", "gx"), None, None),
            P("grp", None),
            P("grp"),
            P("grp"),
            P("grp"),
            P("grp"),
        ),
        out_specs=(
            P(None, ("grp", "gx"), None, None),
            P(None, ("grp", "gx"), None, None),
            P(None, ("grp", "gx"), None, None),
            P(None, ("grp", "gx"), None, None),
            P(("grp", "gx"), None, None),
        ),
        check_vma=False,
    )
```

```python
import functools

import jax
import jax.numpy as jnp
from jax import lax
from jax.experimental import pallas as pl
from jax.experimental.pallas import tpu as pltpu
from jax.sharding import PartitionSpec as P

DT = 0.5
EPS_RANGE = 10.0
STRENGTH_BASE = 0.5
STRENGTH_RANGE = 3.0
DAMPING = 0.2
GAIN_FIELD = 0.25
HIGH = lax.Precision.HIGHEST
KEEP = 1.0 - DAMPING * DT / 2.0
LOSS = 1.0 + DAMPING * DT / 2.0
SHRINK = 1.0 / LOSS


def passed_along(block, axis, distance):
    devices = range(lax.axis_size(axis))
    route = [(i - distance, i) for i in devices if i - distance in devices]
    return lax.ppermute(block, axis, route)


def band_matrix(count, radius):
    rows = jnp.arange(count, dtype=jnp.int32)
    dist = jnp.abs(rows[:, None] - rows[None, :])
    weights = jnp.maximum(radius + 1 - dist, 0).astype(jnp.float32)
    return weights / jnp.sum(weights, axis=1, keepdims=True)


def smooth(wx, wy, planes):
    inner = jnp.einsum("ax,zxy->zay", wx, planes, precision=HIGH)
    return jnp.einsum("zay,by->zab", inner, wy, precision=HIGH)


def smooth_adjoint(wx, wy, planes):
    inner = jnp.einsum("ax,zab->zxb", wx, planes, precision=HIGH)
    return jnp.einsum("zxb,by->zxy", inner, wy, precision=HIGH)


def field_kernel(
    ef, hf, ea, ha, pa, ja, pf, jf, arrived, upper, below, src, mon, amp, first,
    ef_o, hf_o, ea_o, ha_o, ret_o, rho,
):
    depth, width_x, width_y = rho.shape
    slab = arrived.shape[0]
    index = lax.axis_index("gx")
    start = first[0]
    for z in range(depth):
        p = index * depth + z - start
        inside = (p >= 0) & (p < slab)
        rho[z] = jnp.where(inside, arrived[jnp.clip(p, 0, slab - 1)], 0.0)
    row = lax.broadcasted_iota(jnp.int32, (width_x, width_y), 0)
    lane = lax.broadcasted_iota(jnp.int32, (width_x, width_y), 1)

    def ahead_y(f):
        return jnp.where(lane == width_y - 1, 0.0, pltpu.roll(f, width_y - 1, 1))

    def ahead_x(f):
        return jnp.where(row == width_x - 1, 0.0, pltpu.roll(f, width_x - 1, 0))

    def behind_y(f):
        return jnp.where(lane == 0, 0.0, pltpu.roll(f, 1, 1))

    def behind_x(f):
        return jnp.where(row == 0, 0.0, pltpu.roll(f, 1, 0))

    def new_h(e, h, z, ex_up, ey_up):
        ex, ey, ez = e[0, z], e[1, z], e[2, z]
        curl_x = ahead_y(ez) - ez - (ey_up - ey)
        curl_y = ex_up - ex - (ahead_x(ez) - ez)
        curl_z = ahead_x(ey) - ey - (ahead_y(ex) - ex)
        return (h[0, z] - DT * curl_x, h[1, z] - DT * curl_y, h[2, z] - DT * curl_z)

    def lower_h(e, base):
        hx, hy, ex, ey, ez = (below[base + i] for i in range(5))
        curl_x = ahead_y(ez) - ez - (e[1, 0] - ey)
        curl_y = e[0, 0] - ex - (ahead_x(ez) - ez)
        keep = index > 0
        return (
            jnp.where(keep, hx - DT * curl_x, 0.0),
            jnp.where(keep, hy - DT * curl_y, 0.0),
        )

    def new_e(e, p, j, out, z, hn, hn_dn, step, strength):
        hx, hy, hz = hn
        hx_dn, hy_dn = hn_dn
        curl = (
            hz - behind_y(hz) - (hy - hy_dn),
            hx - hx_dn - (hz - behind_x(hz)),
            hy - behind_x(hy) - (hx - behind_y(hx)),
        )
        for c in range(3):
            j_next = (KEEP * j[c, z] + DT * (strength * e[c, z] - p[c, z])) * SHRINK
            out[c, z] = e[c, z] + step * (curl[c] - j_next)

    runs = ((ef, hf, pf, jf, hf_o, ef_o, 0), (ea, ha, pa, ja, ha_o, ea_o, 2))
    prev = [lower_h(ef, 0), lower_h(ea, 5)]
    for z in range(depth):
        density = rho[z]
        step = DT / (1.0 + EPS_RANGE * density)
        strength = STRENGTH_BASE + STRENGTH_RANGE * density
        for r, (e, h, p, j, h_out, e_out, up) in enumerate(runs):
            if z + 1 < depth:
                ex_up, ey_up = e[0, z + 1], e[1, z + 1]
            else:
                ex_up, ey_up = upper[up], upper[up + 1]
            hn = new_h(e, h, z, ex_up, ey_up)
            for c in range(3):
                h_out[c, z] = hn[c]
            new_e(e, p, j, e_out, z, hn, prev[r], step, strength)
            prev[r] = (hn[0], hn[1])

    plane = width_x * width_y
    tile_row = lax.broadcasted_iota(jnp.int32, (8, width_y), 0)
    tile_lane = lax.broadcasted_iota(jnp.int32, (8, width_y), 1)

    def add_at(cell, out, value_of):
        zz = cell // plane
        local = zz - index * depth
        rest = cell - zz * plane
        x = rest // width_y
        y = rest - x * width_y
        x0 = pl.multiple_of((x // 8) * 8, 8)

        @pl.when((local >= 0) & (local < depth))
        def _():
            rows = pl.ds(x0, 8)
            hit = (tile_row == x - x0) & (tile_lane == y)
            step = DT / (1.0 + EPS_RANGE * rho[local, rows, :])
            for c in range(3):
                held = out[c, local, rows, :]
                out[c, local, rows, :] = held + jnp.where(hit, step * value_of(c, local, rows), 0.0)

    for s in range(src.shape[0]):
        add_at(src[s], ef_o, lambda c, local, rows, s=s: amp[s, c])
    for m in range(mon.shape[0]):
        add_at(mon[m], ea_o, lambda c, local, rows: ef[c, local, rows, :])

    for g in range(slab):
        ret_o[g] = jnp.zeros((width_x, width_y), jnp.float32)
    for z in range(depth):
        total = None
        for c in range(3):
            fwd = ef_o[c, z]
            term = ea_o[c, z] * (fwd - ef[c, z] + GAIN_FIELD * fwd)
            total = term if total is None else total + term
        p = index * depth + z - start

        @pl.when((p >= 0) & (p < slab))
        def _():
            ret_o[jnp.clip(p, 0, slab - 1)] = total


def fields(e_forward, h_forward, p_forward, j_forward, e_adjoint, h_adjoint, p_adjoint, j_adjoint,
           arrived, upper, below, source_cell, monitor_cell, source_amp, slab_start):
    shape = e_forward.shape
    depth = shape[1]
    field = jax.ShapeDtypeStruct(shape, jnp.float32)
    vmem = pl.BlockSpec(memory_space=pltpu.VMEM)
    smem = pl.BlockSpec(memory_space=pltpu.SMEM)
    cells = shape[1] * shape[2] * shape[3]
    return pl.pallas_call(
        field_kernel,
        out_shape=(field, field, field, field, jax.ShapeDtypeStruct(arrived.shape, jnp.float32)),
        in_specs=[vmem] * 11 + [smem] * 4,
        out_specs=(vmem,) * 5,
        scratch_shapes=[pltpu.VMEM(shape[1:], jnp.float32)],
        compiler_params=pltpu.CompilerParams(vmem_limit_bytes=56 * 1024 * 1024),
        cost_estimate=pl.CostEstimate(
            flops=200 * cells, bytes_accessed=4 * cells * 40, transcendentals=0
        ),
    )(e_forward, h_forward, e_adjoint, h_adjoint, p_adjoint, j_adjoint, p_forward, j_forward,
      arrived, upper, below, source_cell, monitor_cell, source_amp, slab_start)


def body(
    e_forward,
    h_forward,
    p_forward,
    j_forward,
    e_adjoint,
    h_adjoint,
    p_adjoint,
    j_adjoint,
    design,
    source_amp,
    source_cell,
    monitor_cell,
    slab_start,
    radius,
):
    count = lax.axis_size("gx")
    index = lax.axis_index("gx")
    depth, width_x, width_y = (e_forward.shape[1], e_forward.shape[2], e_forward.shape[3])
    start = slab_start[0]
    wx = band_matrix(width_x, radius[0])
    wy = band_matrix(width_y, radius[0])
    upper = passed_along(jnp.concatenate([e_forward[0:2, 0], e_adjoint[0:2, 0]], 0), "gx", -1)
    below = passed_along(
        jnp.concatenate(
            [h_forward[0:2, -1], e_forward[:, -1], h_adjoint[0:2, -1], e_adjoint[:, -1]], 0
        ),
        "gx",
        1,
    )
    owned = smooth(wx, wy, design)
    holder = (start + index) // depth
    target = (jnp.arange(count, dtype=jnp.int32) == holder).astype(jnp.float32)
    slots = target[:, None, None] * owned
    arrived = lax.all_to_all(slots, "gx", split_axis=0, concat_axis=0, tiled=True)
    ef, hf, ea, ha, returned = fields(
        e_forward, h_forward, p_forward, j_forward, e_adjoint, h_adjoint, p_adjoint, j_adjoint,
        arrived, upper, below, source_cell, monitor_cell, source_amp, slab_start,
    )
    arrived_back = lax.all_to_all(returned, "gx", split_axis=0, concat_axis=0, tiled=True)
    inner = jnp.einsum("ax,jab->xb", wx, arrived_back, precision=HIGH)
    design_grad = jnp.einsum("xb,by->xy", inner, wy, precision=HIGH)[None]
    return (ef, hf, ea, ha, design_grad)


def solution(mesh):
    return jax.shard_map(
        body,
        mesh=mesh,
        in_specs=(
            P(None, ("grp", "gx"), None, None),
            P(None, ("grp", "gx"), None, None),
            P(None, ("grp", "gx"), None, None),
            P(None, ("grp", "gx"), None, None),
            P(None, ("grp", "gx"), None, None),
            P(None, ("grp", "gx"), None, None),
            P(None, ("grp", "gx"), None, None),
            P(None, ("grp", "gx"), None, None),
            P(("grp", "gx"), None, None),
            P("grp", None),
            P("grp"),
            P("grp"),
            P("grp"),
            P("grp"),
        ),
        out_specs=(
            P(None, ("grp", "gx"), None, None),
            P(None, ("grp", "gx"), None, None),
            P(None, ("grp", "gx"), None, None),
            P(None, ("grp", "gx"), None, None),
            P(("grp", "gx"), None, None),
        ),
        check_vma=False,
    )
```

```python
import functools

import jax
import jax.numpy as jnp
from jax import lax
from jax.experimental import pallas as pl
from jax.experimental.pallas import tpu as pltpu
from jax.sharding import PartitionSpec as P

DT = 0.5
EPS_RANGE = 10.0
STRENGTH_BASE = 0.5
STRENGTH_RANGE = 3.0
DAMPING = 0.2
GAIN_FIELD = 0.25
HIGH = lax.Precision.HIGHEST
KEEP = 1.0 - DAMPING * DT / 2.0
LOSS = 1.0 + DAMPING * DT / 2.0
SHRINK = 1.0 / LOSS


def passed_along(block, axis, distance):
    devices = range(lax.axis_size(axis))
    route = [(i - distance, i) for i in devices if i - distance in devices]
    return lax.ppermute(block, axis, route)


def band_matrix(count, radius):
    rows = jnp.arange(count, dtype=jnp.int32)
    dist = jnp.abs(rows[:, None] - rows[None, :])
    weights = jnp.maximum(radius + 1 - dist, 0).astype(jnp.float32)
    return weights / jnp.sum(weights, axis=1, keepdims=True)


def smooth(wx, wy, planes):
    inner = jnp.einsum("ax,zxy->zay", wx, planes, precision=HIGH)
    return jnp.einsum("zay,by->zab", inner, wy, precision=HIGH)


def smooth_adjoint(wx, wy, planes):
    inner = jnp.einsum("ax,zab->zxb", wx, planes, precision=HIGH)
    return jnp.einsum("zxb,by->zxy", inner, wy, precision=HIGH)


def field_kernel(
    ef, hf, pf, jf, ea, ha, pa, ja, arrived, upper, below, src, mon, amp, first,
    ef_o, hf_o, ea_o, ha_o, ret_o, rho,
):
    depth, width_x, width_y = rho.shape
    slab = arrived.shape[0]
    index = lax.axis_index("gx")
    start = first[0]
    for z in range(depth):
        p = index * depth + z - start
        inside = (p >= 0) & (p < slab)
        rho[z] = jnp.where(inside, arrived[jnp.clip(p, 0, slab - 1)], 0.0)
    row = lax.broadcasted_iota(jnp.int32, (width_x, width_y), 0)
    lane = lax.broadcasted_iota(jnp.int32, (width_x, width_y), 1)

    def ahead_y(f):
        return jnp.where(lane == width_y - 1, 0.0, pltpu.roll(f, width_y - 1, 1))

    def ahead_x(f):
        return jnp.where(row == width_x - 1, 0.0, pltpu.roll(f, width_x - 1, 0))

    def behind_y(f):
        return jnp.where(lane == 0, 0.0, pltpu.roll(f, 1, 1))

    def behind_x(f):
        return jnp.where(row == 0, 0.0, pltpu.roll(f, 1, 0))

    def new_h(e, h, z, ex_up, ey_up):
        ex, ey, ez = e[0, z], e[1, z], e[2, z]
        curl_x = ahead_y(ez) - ez - (ey_up - ey)
        curl_y = ex_up - ex - (ahead_x(ez) - ez)
        curl_z = ahead_x(ey) - ey - (ahead_y(ex) - ex)
        return (h[0, z] - DT * curl_x, h[1, z] - DT * curl_y, h[2, z] - DT * curl_z)

    def lower_h(e, base):
        hx, hy, ex, ey, ez = (below[base + i] for i in range(5))
        curl_x = ahead_y(ez) - ez - (e[1, 0] - ey)
        curl_y = e[0, 0] - ex - (ahead_x(ez) - ez)
        keep = index > 0
        return (
            jnp.where(keep, hx - DT * curl_x, 0.0),
            jnp.where(keep, hy - DT * curl_y, 0.0),
        )

    def new_e(e, p, j, out, z, hn, hn_dn, step, strength):
        hx, hy, hz = hn
        hx_dn, hy_dn = hn_dn
        curl = (
            hz - behind_y(hz) - (hy - hy_dn),
            hx - hx_dn - (hz - behind_x(hz)),
            hy - behind_x(hy) - (hx - behind_y(hx)),
        )
        for c in range(3):
            j_next = (KEEP * j[c, z] + DT * (strength * e[c, z] - p[c, z])) * SHRINK
            out[c, z] = e[c, z] + step * (curl[c] - j_next)

    runs = ((ef, hf, pf, jf, hf_o, ef_o, 0), (ea, ha, pa, ja, ha_o, ea_o, 2))
    prev = [lower_h(ef, 0), lower_h(ea, 5)]
    for z in range(depth):
        density = rho[z]
        step = DT / (1.0 + EPS_RANGE * density)
        strength = STRENGTH_BASE + STRENGTH_RANGE * density
        for r, (e, h, p, j, h_out, e_out, up) in enumerate(runs):
            if z + 1 < depth:
                ex_up, ey_up = e[0, z + 1], e[1, z + 1]
            else:
                ex_up, ey_up = upper[up], upper[up + 1]
            hn = new_h(e, h, z, ex_up, ey_up)
            for c in range(3):
                h_out[c, z] = hn[c]
            new_e(e, p, j, e_out, z, hn, prev[r], step, strength)
            prev[r] = (hn[0], hn[1])

    plane = width_x * width_y
    tile_row = lax.broadcasted_iota(jnp.int32, (8, width_y), 0)
    tile_lane = lax.broadcasted_iota(jnp.int32, (8, width_y), 1)

    def add_at(cell, out, value_of):
        zz = cell // plane
        local = zz - index * depth
        rest = cell - zz * plane
        x = rest // width_y
        y = rest - x * width_y
        x0 = pl.multiple_of((x // 8) * 8, 8)

        @pl.when((local >= 0) & (local < depth))
        def _():
            rows = pl.ds(x0, 8)
            hit = (tile_row == x - x0) & (tile_lane == y)
            step = DT / (1.0 + EPS_RANGE * rho[local, rows, :])
            for c in range(3):
                held = out[c, local, rows, :]
                out[c, local, rows, :] = held + jnp.where(hit, step * value_of(c, local, rows), 0.0)

    for s in range(src.shape[0]):
        add_at(src[s], ef_o, lambda c, local, rows, s=s: amp[s, c])
    for m in range(mon.shape[0]):
        add_at(mon[m], ea_o, lambda c, local, rows: ef[c, local, rows, :])

    for g in range(slab):
        ret_o[g] = jnp.zeros((width_x, width_y), jnp.float32)
    for z in range(depth):
        total = None
        for c in range(3):
            fwd = ef_o[c, z]
            term = ea_o[c, z] * (fwd - ef[c, z] + GAIN_FIELD * fwd)
            total = term if total is None else total + term
        p = index * depth + z - start

        @pl.when((p >= 0) & (p < slab))
        def _():
            ret_o[jnp.clip(p, 0, slab - 1)] = total


def fields(e_forward, h_forward, p_forward, j_forward, e_adjoint, h_adjoint, p_adjoint, j_adjoint,
           arrived, upper, below, source_cell, monitor_cell, source_amp, slab_start):
    shape = e_forward.shape
    depth = shape[1]
    field = jax.ShapeDtypeStruct(shape, jnp.float32)
    vmem = pl.BlockSpec(memory_space=pltpu.VMEM)
    smem = pl.BlockSpec(memory_space=pltpu.SMEM)
    cells = shape[1] * shape[2] * shape[3]
    return pl.pallas_call(
        field_kernel,
        out_shape=(field, field, field, field, jax.ShapeDtypeStruct(arrived.shape, jnp.float32)),
        in_specs=[vmem] * 11 + [smem] * 4,
        out_specs=(vmem,) * 5,
        scratch_shapes=[pltpu.VMEM(shape[1:], jnp.float32)],
        compiler_params=pltpu.CompilerParams(vmem_limit_bytes=48 * 1024 * 1024),
        cost_estimate=pl.CostEstimate(
            flops=200 * cells, bytes_accessed=4 * cells * 40, transcendentals=0
        ),
    )(e_forward, h_forward, p_forward, j_forward, e_adjoint, h_adjoint, p_adjoint, j_adjoint,
      arrived, upper, below, source_cell, monitor_cell, source_amp, slab_start)


def body(
    e_forward,
    h_forward,
    p_forward,
    j_forward,
    e_adjoint,
    h_adjoint,
    p_adjoint,
    j_adjoint,
    design,
    source_amp,
    source_cell,
    monitor_cell,
    slab_start,
    radius,
):
    count = lax.axis_size("gx")
    index = lax.axis_index("gx")
    depth, width_x, width_y = (e_forward.shape[1], e_forward.shape[2], e_forward.shape[3])
    start = slab_start[0]
    wx = band_matrix(width_x, radius[0])
    wy = band_matrix(width_y, radius[0])
    upper = passed_along(jnp.concatenate([e_forward[0:2, 0], e_adjoint[0:2, 0]], 0), "gx", -1)
    below = passed_along(
        jnp.concatenate(
            [h_forward[0:2, -1], e_forward[:, -1], h_adjoint[0:2, -1], e_adjoint[:, -1]], 0
        ),
        "gx",
        1,
    )
    owned = smooth(wx, wy, design)
    slots = jnp.broadcast_to(owned, (count,) + owned.shape[1:])
    arrived = lax.all_to_all(slots, "gx", split_axis=0, concat_axis=0, tiled=True)
    ef, hf, ea, ha, returned = fields(
        e_forward, h_forward, p_forward, j_forward, e_adjoint, h_adjoint, p_adjoint, j_adjoint,
        arrived, upper, below, source_cell, monitor_cell, source_amp, slab_start,
    )
    arrived_back = lax.all_to_all(returned, "gx", split_axis=0, concat_axis=0, tiled=True)
    inner = jnp.einsum("ax,jab->xb", wx, arrived_back, precision=HIGH)
    design_grad = jnp.einsum("xb,by->xy", inner, wy, precision=HIGH)[None]
    return (ef, hf, ea, ha, design_grad)


def solution(mesh):
    return jax.shard_map(
        body,
        mesh=mesh,
        in_specs=(
            P(None, ("grp", "gx"), None, None),
            P(None, ("grp", "gx"), None, None),
            P(None, ("grp", "gx"), None, None),
            P(None, ("grp", "gx"), None, None),
            P(None, ("grp", "gx"), None, None),
            P(None, ("grp", "gx"), None, None),
            P(None, ("grp", "gx"), None, None),
            P(None, ("grp", "gx"), None, None),
            P(("grp", "gx"), None, None),
            P("grp", None),
            P("grp"),
            P("grp"),
            P("grp"),
            P("grp"),
        ),
        out_specs=(
            P(None, ("grp", "gx"), None, None),
            P(None, ("grp", "gx"), None, None),
            P(None, ("grp", "gx"), None, None),
            P(None, ("grp", "gx"), None, None),
            P(("grp", "gx"), None, None),
        ),
        check_vma=False,
    )
```

```python
import functools

import jax
import jax.numpy as jnp
from jax import lax
from jax.experimental import pallas as pl
from jax.experimental.pallas import tpu as pltpu
from jax.sharding import PartitionSpec as P

DT = 0.5
EPS_RANGE = 10.0
STRENGTH_BASE = 0.5
STRENGTH_RANGE = 3.0
DAMPING = 0.2
GAIN_FIELD = 0.25
HIGH = lax.Precision.HIGHEST
KEEP = 1.0 - DAMPING * DT / 2.0
LOSS = 1.0 + DAMPING * DT / 2.0
SHRINK = 1.0 / LOSS


def passed_along(block, axis, distance):
    devices = range(lax.axis_size(axis))
    route = [(i - distance, i) for i in devices if i - distance in devices]
    return lax.ppermute(block, axis, route)


def band_matrix(count, radius):
    rows = jnp.arange(count, dtype=jnp.int32)
    dist = jnp.abs(rows[:, None] - rows[None, :])
    weights = jnp.maximum(radius + 1 - dist, 0).astype(jnp.float32)
    return weights / jnp.sum(weights, axis=1, keepdims=True)


def smooth(wx, wy, planes):
    inner = jnp.einsum("ax,zxy->zay", wx, planes, precision=HIGH)
    return jnp.einsum("zay,by->zab", inner, wy, precision=HIGH)


def smooth_adjoint(wx, wy, planes):
    inner = jnp.einsum("ax,zab->zxb", wx, planes, precision=HIGH)
    return jnp.einsum("zxb,by->zxy", inner, wy, precision=HIGH)


def shifts(width_x, width_y):
    row = lax.broadcasted_iota(jnp.int32, (width_x, width_y), 0)
    lane = lax.broadcasted_iota(jnp.int32, (width_x, width_y), 1)

    def ahead_y(f):
        return jnp.where(lane == width_y - 1, 0.0, pltpu.roll(f, width_y - 1, 1))

    def ahead_x(f):
        return jnp.where(row == width_x - 1, 0.0, pltpu.roll(f, width_x - 1, 0))

    def behind_y(f):
        return jnp.where(lane == 0, 0.0, pltpu.roll(f, 1, 1))

    def behind_x(f):
        return jnp.where(row == 0, 0.0, pltpu.roll(f, 1, 0))

    return ahead_y, ahead_x, behind_y, behind_x


def h_kernel(ef, hf, ea, ha, upper, below, hf_o, ha_o, lower):
    _, depth, width_x, width_y = ef.shape
    ahead_y, ahead_x, _, _ = shifts(width_x, width_y)
    keep = lax.axis_index("gx") > 0
    for r, (e, h, h_out) in enumerate(((ef, hf, hf_o), (ea, ha, ha_o))):
        hx, hy, ex, ey, ez = (below[5 * r + i] for i in range(5))
        curl_x = ahead_y(ez) - ez - (e[1, 0] - ey)
        curl_y = e[0, 0] - ex - (ahead_x(ez) - ez)
        lower[2 * r] = jnp.where(keep, hx - DT * curl_x, 0.0)
        lower[2 * r + 1] = jnp.where(keep, hy - DT * curl_y, 0.0)
        for z in range(depth):
            if z + 1 < depth:
                ex_up, ey_up = e[0, z + 1], e[1, z + 1]
            else:
                ex_up, ey_up = upper[2 * r], upper[2 * r + 1]
            ex, ey, ez = e[0, z], e[1, z], e[2, z]
            h_out[0, z] = h[0, z] - DT * (ahead_y(ez) - ez - (ey_up - ey))
            h_out[1, z] = h[1, z] - DT * (ex_up - ex - (ahead_x(ez) - ez))
            h_out[2, z] = h[2, z] - DT * (ahead_x(ey) - ey - (ahead_y(ex) - ex))


def e_kernel(
    ef, pf, jf, ea, pa, ja, hfn, han, lower, arrived, src, mon, amp, first,
    ef_o, ea_o, ret_o, rho,
):
    depth, width_x, width_y = rho.shape
    slab = arrived.shape[0]
    index = lax.axis_index("gx")
    start = first[0]
    for z in range(depth):
        p = index * depth + z - start
        inside = (p >= 0) & (p < slab)
        rho[z] = jnp.where(inside, arrived[jnp.clip(p, 0, slab - 1)], 0.0)
    _, _, behind_y, behind_x = shifts(width_x, width_y)

    runs = ((ef, pf, jf, hfn, ef_o), (ea, pa, ja, han, ea_o))
    for z in range(depth):
        density = rho[z]
        step = DT / (1.0 + EPS_RANGE * density)
        strength = STRENGTH_BASE + STRENGTH_RANGE * density
        for r, (e, p, j, hn, e_out) in enumerate(runs):
            hx, hy, hz = hn[0, z], hn[1, z], hn[2, z]
            if z > 0:
                hx_dn, hy_dn = hn[0, z - 1], hn[1, z - 1]
            else:
                hx_dn, hy_dn = lower[2 * r], lower[2 * r + 1]
            curl = (
                hz - behind_y(hz) - (hy - hy_dn),
                hx - hx_dn - (hz - behind_x(hz)),
                hy - behind_x(hy) - (hx - behind_y(hx)),
            )
            for c in range(3):
                j_next = (KEEP * j[c, z] + DT * (strength * e[c, z] - p[c, z])) * SHRINK
                e_out[c, z] = e[c, z] + step * (curl[c] - j_next)

    plane = width_x * width_y
    tile_row = lax.broadcasted_iota(jnp.int32, (8, width_y), 0)
    tile_lane = lax.broadcasted_iota(jnp.int32, (8, width_y), 1)

    def add_at(cell, out, value_of):
        zz = cell // plane
        local = zz - index * depth
        rest = cell - zz * plane
        x = rest // width_y
        y = rest - x * width_y
        x0 = pl.multiple_of((x // 8) * 8, 8)

        @pl.when((local >= 0) & (local < depth))
        def _():
            rows = pl.ds(x0, 8)
            hit = (tile_row == x - x0) & (tile_lane == y)
            gain = DT / (1.0 + EPS_RANGE * rho[local, rows, :])
            for c in range(3):
                held = out[c, local, rows, :]
                out[c, local, rows, :] = held + jnp.where(hit, gain * value_of(c, local, rows), 0.0)

    for s in range(src.shape[0]):
        add_at(src[s], ef_o, lambda c, local, rows, s=s: amp[s, c])
    for m in range(mon.shape[0]):
        add_at(mon[m], ea_o, lambda c, local, rows: ef[c, local, rows, :])

    for g in range(slab):
        ret_o[g] = jnp.zeros((width_x, width_y), jnp.float32)
    for z in range(depth):
        total = None
        for c in range(3):
            fwd = ef_o[c, z]
            term = ea_o[c, z] * (fwd - ef[c, z] + GAIN_FIELD * fwd)
            total = term if total is None else total + term
        p = index * depth + z - start

        @pl.when((p >= 0) & (p < slab))
        def _():
            ret_o[jnp.clip(p, 0, slab - 1)] = total


def fields(e_forward, h_forward, p_forward, j_forward, e_adjoint, h_adjoint, p_adjoint, j_adjoint,
           arrived, upper, below, source_cell, monitor_cell, source_amp, slab_start):
    shape = e_forward.shape
    field = jax.ShapeDtypeStruct(shape, jnp.float32)
    vmem = pl.BlockSpec(memory_space=pltpu.VMEM)
    smem = pl.BlockSpec(memory_space=pltpu.SMEM)
    cells = shape[1] * shape[2] * shape[3]
    hf, ha, lower = pl.pallas_call(
        h_kernel,
        out_shape=(field, field, jax.ShapeDtypeStruct((4,) + shape[2:], jnp.float32)),
        in_specs=[vmem] * 6,
        out_specs=(vmem,) * 3,
        compiler_params=pltpu.CompilerParams(vmem_limit_bytes=12 * 1024 * 1024),
        cost_estimate=pl.CostEstimate(
            flops=60 * cells, bytes_accessed=4 * cells * 18, transcendentals=0
        ),
    )(e_forward, h_forward, e_adjoint, h_adjoint, upper, below)
    ef, ea, returned = pl.pallas_call(
        e_kernel,
        out_shape=(field, field, jax.ShapeDtypeStruct(arrived.shape, jnp.float32)),
        in_specs=[vmem] * 10 + [smem] * 4,
        out_specs=(vmem,) * 3,
        scratch_shapes=[pltpu.VMEM(shape[1:], jnp.float32)],
        compiler_params=pltpu.CompilerParams(vmem_limit_bytes=56 * 1024 * 1024),
        cost_estimate=pl.CostEstimate(
            flops=140 * cells, bytes_accessed=4 * cells * 30, transcendentals=0
        ),
    )(e_forward, p_forward, j_forward, e_adjoint, p_adjoint, j_adjoint, hf, ha, lower, arrived,
      source_cell, monitor_cell, source_amp, slab_start)
    return ef, hf, ea, ha, returned


def body(
    e_forward,
    h_forward,
    p_forward,
    j_forward,
    e_adjoint,
    h_adjoint,
    p_adjoint,
    j_adjoint,
    design,
    source_amp,
    source_cell,
    monitor_cell,
    slab_start,
    radius,
):
    count = lax.axis_size("gx")
    index = lax.axis_index("gx")
    depth, width_x, width_y = (e_forward.shape[1], e_forward.shape[2], e_forward.shape[3])
    start = slab_start[0]
    wx = band_matrix(width_x, radius[0])
    wy = band_matrix(width_y, radius[0])
    upper = passed_along(jnp.concatenate([e_forward[0:2, 0], e_adjoint[0:2, 0]], 0), "gx", -1)
    below = passed_along(
        jnp.concatenate(
            [h_forward[0:2, -1], e_forward[:, -1], h_adjoint[0:2, -1], e_adjoint[:, -1]], 0
        ),
        "gx",
        1,
    )
    owned = smooth(wx, wy, design)
    slots = jnp.broadcast_to(owned, (count,) + owned.shape[1:])
    arrived = lax.all_to_all(slots, "gx", split_axis=0, concat_axis=0, tiled=True)
    ef, hf, ea, ha, returned = fields(
        e_forward, h_forward, p_forward, j_forward, e_adjoint, h_adjoint, p_adjoint, j_adjoint,
        arrived, upper, below, source_cell, monitor_cell, source_amp, slab_start,
    )
    arrived_back = lax.all_to_all(returned, "gx", split_axis=0, concat_axis=0, tiled=True)
    inner = jnp.einsum("ax,jab->xb", wx, arrived_back, precision=HIGH)
    design_grad = jnp.einsum("xb,by->xy", inner, wy, precision=HIGH)[None]
    return (ef, hf, ea, ha, design_grad)


def solution(mesh):
    return jax.shard_map(
        body,
        mesh=mesh,
        in_specs=(
            P(None, ("grp", "gx"), None, None),
            P(None, ("grp", "gx"), None, None),
            P(None, ("grp", "gx"), None, None),
            P(None, ("grp", "gx"), None, None),
            P(None, ("grp", "gx"), None, None),
            P(None, ("grp", "gx"), None, None),
            P(None, ("grp", "gx"), None, None),
            P(None, ("grp", "gx"), None, None),
            P(("grp", "gx"), None, None),
            P("grp", None),
            P("grp"),
            P("grp"),
            P("grp"),
            P("grp"),
        ),
        out_specs=(
            P(None, ("grp", "gx"), None, None),
            P(None, ("grp", "gx"), None, None),
            P(None, ("grp", "gx"), None, None),
            P(None, ("grp", "gx"), None, None),
            P(("grp", "gx"), None, None),
        ),
        check_vma=False,
    )
```

```python
import functools

import jax
import jax.numpy as jnp
from jax import lax
from jax.experimental import pallas as pl
from jax.experimental.pallas import tpu as pltpu
from jax.sharding import PartitionSpec as P

DT = 0.5
EPS_RANGE = 10.0
STRENGTH_BASE = 0.5
STRENGTH_RANGE = 3.0
DAMPING = 0.2
GAIN_FIELD = 0.25
HIGH = lax.Precision.HIGHEST
KEEP = 1.0 - DAMPING * DT / 2.0
LOSS = 1.0 + DAMPING * DT / 2.0
SHRINK = 1.0 / LOSS


def passed_along(block, axis, distance):
    devices = range(lax.axis_size(axis))
    route = [(i - distance, i) for i in devices if i - distance in devices]
    return lax.ppermute(block, axis, route)


def band_matrix(count, radius):
    rows = jnp.arange(count, dtype=jnp.int32)
    dist = jnp.abs(rows[:, None] - rows[None, :])
    weights = jnp.maximum(radius + 1 - dist, 0).astype(jnp.float32)
    return weights / jnp.sum(weights, axis=1, keepdims=True)


def smooth(wx, wy, planes):
    inner = jnp.einsum("ax,zxy->zay", wx, planes, precision=HIGH)
    return jnp.einsum("zay,by->zab", inner, wy, precision=HIGH)


def smooth_adjoint(wx, wy, planes):
    inner = jnp.einsum("ax,zab->zxb", wx, planes, precision=HIGH)
    return jnp.einsum("zxb,by->zxy", inner, wy, precision=HIGH)


def shifts(width_x, width_y):
    row = lax.broadcasted_iota(jnp.int32, (width_x, width_y), 0)
    lane = lax.broadcasted_iota(jnp.int32, (width_x, width_y), 1)

    def ahead_y(f):
        return jnp.where(lane == width_y - 1, 0.0, pltpu.roll(f, width_y - 1, 1))

    def ahead_x(f):
        return jnp.where(row == width_x - 1, 0.0, pltpu.roll(f, width_x - 1, 0))

    def behind_y(f):
        return jnp.where(lane == 0, 0.0, pltpu.roll(f, 1, 1))

    def behind_x(f):
        return jnp.where(row == 0, 0.0, pltpu.roll(f, 1, 0))

    return ahead_y, ahead_x, behind_y, behind_x


def h_kernel(ef, hf, pf, jf, ea, ha, pa, ja, upper, below, hf_o, ha_o, qf_o, qa_o):
    _, depth, width_x, width_y = ef.shape
    ahead_y, ahead_x, behind_y, behind_x = shifts(width_x, width_y)
    keep = lax.axis_index("gx") > 0
    runs = ((ef, hf, pf, jf, hf_o, qf_o), (ea, ha, pa, ja, ha_o, qa_o))
    for r, (e, h, p, j, h_out, q_out) in enumerate(runs):
        hx, hy, ex, ey, ez = (below[5 * r + i] for i in range(5))
        curl_x = ahead_y(ez) - ez - (e[1, 0] - ey)
        curl_y = e[0, 0] - ex - (ahead_x(ez) - ez)
        hx_dn = jnp.where(keep, hx - DT * curl_x, 0.0)
        hy_dn = jnp.where(keep, hy - DT * curl_y, 0.0)
        for z in range(depth):
            if z + 1 < depth:
                ex_up, ey_up = e[0, z + 1], e[1, z + 1]
            else:
                ex_up, ey_up = upper[2 * r], upper[2 * r + 1]
            ex, ey, ez = e[0, z], e[1, z], e[2, z]
            hx = h[0, z] - DT * (ahead_y(ez) - ez - (ey_up - ey))
            hy = h[1, z] - DT * (ex_up - ex - (ahead_x(ez) - ez))
            hz = h[2, z] - DT * (ahead_x(ey) - ey - (ahead_y(ex) - ex))
            h_out[0, z] = hx
            h_out[1, z] = hy
            h_out[2, z] = hz
            curl = (
                hz - behind_y(hz) - (hy - hy_dn),
                hx - hx_dn - (hz - behind_x(hz)),
                hy - behind_x(hy) - (hx - behind_y(hx)),
            )
            for c in range(3):
                q_out[c, z] = curl[c] - (KEEP * j[c, z] - DT * p[c, z]) * SHRINK
            hx_dn, hy_dn = hx, hy


def e_kernel(ef, qf, ea, qa, arrived, src, mon, amp, first, ef_o, ea_o, ret_o, rho):
    depth, width_x, width_y = rho.shape
    slab = arrived.shape[0]
    index = lax.axis_index("gx")
    start = first[0]
    for z in range(depth):
        p = index * depth + z - start
        inside = (p >= 0) & (p < slab)
        rho[z] = jnp.where(inside, arrived[jnp.clip(p, 0, slab - 1)], 0.0)

    for z in range(depth):
        density = rho[z]
        step = DT / (1.0 + EPS_RANGE * density)
        strength = STRENGTH_BASE + STRENGTH_RANGE * density
        for e, q, e_out in ((ef, qf, ef_o), (ea, qa, ea_o)):
            for c in range(3):
                e_out[c, z] = e[c, z] + step * (q[c, z] - DT * SHRINK * (strength * e[c, z]))

    plane = width_x * width_y
    tile_row = lax.broadcasted_iota(jnp.int32, (8, width_y), 0)
    tile_lane = lax.broadcasted_iota(jnp.int32, (8, width_y), 1)

    def add_at(cell, out, value_of):
        zz = cell // plane
        local = zz - index * depth
        rest = cell - zz * plane
        x = rest // width_y
        y = rest - x * width_y
        x0 = pl.multiple_of((x // 8) * 8, 8)

        @pl.when((local >= 0) & (local < depth))
        def _():
            rows = pl.ds(x0, 8)
            hit = (tile_row == x - x0) & (tile_lane == y)
            gain = DT / (1.0 + EPS_RANGE * rho[local, rows, :])
            for c in range(3):
                held = out[c, local, rows, :]
                out[c, local, rows, :] = held + jnp.where(hit, gain * value_of(c, local, rows), 0.0)

    for s in range(src.shape[0]):
        add_at(src[s], ef_o, lambda c, local, rows, s=s: amp[s, c])
    for m in range(mon.shape[0]):
        add_at(mon[m], ea_o, lambda c, local, rows: ef[c, local, rows, :])

    for g in range(slab):
        ret_o[g] = jnp.zeros((width_x, width_y), jnp.float32)
    for z in range(depth):
        total = None
        for c in range(3):
            fwd = ef_o[c, z]
            term = ea_o[c, z] * (fwd - ef[c, z] + GAIN_FIELD * fwd)
            total = term if total is None else total + term
        p = index * depth + z - start

        @pl.when((p >= 0) & (p < slab))
        def _():
            ret_o[jnp.clip(p, 0, slab - 1)] = total


def fields(e_forward, h_forward, p_forward, j_forward, e_adjoint, h_adjoint, p_adjoint, j_adjoint,
           arrived, upper, below, source_cell, monitor_cell, source_amp, slab_start):
    shape = e_forward.shape
    field = jax.ShapeDtypeStruct(shape, jnp.float32)
    vmem = pl.BlockSpec(memory_space=pltpu.VMEM)
    smem = pl.BlockSpec(memory_space=pltpu.SMEM)
    cells = shape[1] * shape[2] * shape[3]
    hf, ha, qf, qa = pl.pallas_call(
        h_kernel,
        out_shape=(field,) * 4,
        in_specs=[vmem] * 10,
        out_specs=(vmem,) * 4,
        compiler_params=pltpu.CompilerParams(vmem_limit_bytes=24 * 1024 * 1024),
        cost_estimate=pl.CostEstimate(
            flops=120 * cells, bytes_accessed=4 * cells * 36, transcendentals=0
        ),
    )(e_forward, h_forward, p_forward, j_forward, e_adjoint, h_adjoint, p_adjoint, j_adjoint,
      upper, below)
    ef, ea, returned = pl.pallas_call(
        e_kernel,
        out_shape=(field, field, jax.ShapeDtypeStruct(arrived.shape, jnp.float32)),
        in_specs=[vmem] * 5 + [smem] * 4,
        out_specs=(vmem,) * 3,
        scratch_shapes=[pltpu.VMEM(shape[1:], jnp.float32)],
        compiler_params=pltpu.CompilerParams(vmem_limit_bytes=56 * 1024 * 1024),
        cost_estimate=pl.CostEstimate(
            flops=40 * cells, bytes_accessed=4 * cells * 20, transcendentals=0
        ),
    )(e_forward, qf, e_adjoint, qa, arrived, source_cell, monitor_cell, source_amp, slab_start)
    return ef, hf, ea, ha, returned


def body(
    e_forward,
    h_forward,
    p_forward,
    j_forward,
    e_adjoint,
    h_adjoint,
    p_adjoint,
    j_adjoint,
    design,
    source_amp,
    source_cell,
    monitor_cell,
    slab_start,
    radius,
):
    count = lax.axis_size("gx")
    index = lax.axis_index("gx")
    depth, width_x, width_y = (e_forward.shape[1], e_forward.shape[2], e_forward.shape[3])
    start = slab_start[0]
    wx = band_matrix(width_x, radius[0])
    wy = band_matrix(width_y, radius[0])
    upper = passed_along(jnp.concatenate([e_forward[0:2, 0], e_adjoint[0:2, 0]], 0), "gx", -1)
    below = passed_along(
        jnp.concatenate(
            [h_forward[0:2, -1], e_forward[:, -1], h_adjoint[0:2, -1], e_adjoint[:, -1]], 0
        ),
        "gx",
        1,
    )
    owned = smooth(wx, wy, design)
    slots = jnp.broadcast_to(owned, (count,) + owned.shape[1:])
    arrived = lax.all_to_all(slots, "gx", split_axis=0, concat_axis=0, tiled=True)
    ef, hf, ea, ha, returned = fields(
        e_forward, h_forward, p_forward, j_forward, e_adjoint, h_adjoint, p_adjoint, j_adjoint,
        arrived, upper, below, source_cell, monitor_cell, source_amp, slab_start,
    )
    arrived_back = lax.all_to_all(returned, "gx", split_axis=0, concat_axis=0, tiled=True)
    inner = jnp.einsum("ax,jab->xb", wx, arrived_back, precision=HIGH)
    design_grad = jnp.einsum("xb,by->xy", inner, wy, precision=HIGH)[None]
    return (ef, hf, ea, ha, design_grad)


def solution(mesh):
    return jax.shard_map(
        body,
        mesh=mesh,
        in_specs=(
            P(None, ("grp", "gx"), None, None),
            P(None, ("grp", "gx"), None, None),
            P(None, ("grp", "gx"), None, None),
            P(None, ("grp", "gx"), None, None),
            P(None, ("grp", "gx"), None, None),
            P(None, ("grp", "gx"), None, None),
            P(None, ("grp", "gx"), None, None),
            P(None, ("grp", "gx"), None, None),
            P(("grp", "gx"), None, None),
            P("grp", None),
            P("grp"),
            P("grp"),
            P("grp"),
            P("grp"),
        ),
        out_specs=(
            P(None, ("grp", "gx"), None, None),
            P(None, ("grp", "gx"), None, None),
            P(None, ("grp", "gx"), None, None),
            P(None, ("grp", "gx"), None, None),
            P(("grp", "gx"), None, None),
        ),
        check_vma=False,
    )
```

```python
import functools

import jax
import jax.numpy as jnp
from jax import lax
from jax.experimental import pallas as pl
from jax.experimental.pallas import tpu as pltpu
from jax.sharding import PartitionSpec as P

DT = 0.5
EPS_RANGE = 10.0
STRENGTH_BASE = 0.5
STRENGTH_RANGE = 3.0
DAMPING = 0.2
GAIN_FIELD = 0.25
HIGH = lax.Precision.HIGHEST
KEEP = 1.0 - DAMPING * DT / 2.0
LOSS = 1.0 + DAMPING * DT / 2.0
SHRINK = 1.0 / LOSS


def passed_along(block, axis, distance):
    devices = range(lax.axis_size(axis))
    route = [(i - distance, i) for i in devices if i - distance in devices]
    return lax.ppermute(block, axis, route)


def band_matrix(count, radius):
    rows = jnp.arange(count, dtype=jnp.int32)
    dist = jnp.abs(rows[:, None] - rows[None, :])
    weights = jnp.maximum(radius + 1 - dist, 0).astype(jnp.float32)
    return weights / jnp.sum(weights, axis=1, keepdims=True)


def smooth(wx, wy, planes):
    inner = jnp.einsum("ax,zxy->zay", wx, planes, precision=HIGH)
    return jnp.einsum("zay,by->zab", inner, wy, precision=HIGH)


def smooth_adjoint(wx, wy, planes):
    inner = jnp.einsum("ax,zab->zxb", wx, planes, precision=HIGH)
    return jnp.einsum("zxb,by->zxy", inner, wy, precision=HIGH)


def split_cell(cell, width_x, width_y):
    plane = width_x * width_y
    if plane & (plane - 1) == 0 and width_y & (width_y - 1) == 0:
        zz = lax.shift_right_arithmetic(cell, plane.bit_length() - 1)
        rest = lax.bitwise_and(cell, plane - 1)
        x = lax.shift_right_arithmetic(rest, width_y.bit_length() - 1)
        return zz, x, lax.bitwise_and(rest, width_y - 1)
    zz = cell // plane
    rest = cell - zz * plane
    x = rest // width_y
    return zz, x, rest - x * width_y


def field_kernel(
    ef, hf, pf, jf, ea, ha, pa, ja, arrived, upper, below, src, mon, amp, first,
    ef_o, hf_o, ea_o, ha_o, ret_o, rho,
):
    depth, width_x, width_y = rho.shape
    slab = arrived.shape[0]
    index = lax.axis_index("gx")
    start = first[0]
    for z in range(depth):
        p = index * depth + z - start
        inside = (p >= 0) & (p < slab)
        rho[z] = jnp.where(inside, arrived[jnp.clip(p, 0, slab - 1)], 0.0)
    row = lax.broadcasted_iota(jnp.int32, (width_x, width_y), 0)
    lane = lax.broadcasted_iota(jnp.int32, (width_x, width_y), 1)

    def ahead_y(f):
        return jnp.where(lane == width_y - 1, 0.0, pltpu.roll(f, width_y - 1, 1))

    def ahead_x(f):
        return jnp.where(row == width_x - 1, 0.0, pltpu.roll(f, width_x - 1, 0))

    def behind_y(f):
        return jnp.where(lane == 0, 0.0, pltpu.roll(f, 1, 1))

    def behind_x(f):
        return jnp.where(row == 0, 0.0, pltpu.roll(f, 1, 0))

    def new_h(e, h, z, ex_up, ey_up):
        ex, ey, ez = e[0, z], e[1, z], e[2, z]
        curl_x = ahead_y(ez) - ez - (ey_up - ey)
        curl_y = ex_up - ex - (ahead_x(ez) - ez)
        curl_z = ahead_x(ey) - ey - (ahead_y(ex) - ex)
        return (h[0, z] - DT * curl_x, h[1, z] - DT * curl_y, h[2, z] - DT * curl_z)

    def lower_h(e, base):
        hx, hy, ex, ey, ez = (below[base + i] for i in range(5))
        curl_x = ahead_y(ez) - ez - (e[1, 0] - ey)
        curl_y = e[0, 0] - ex - (ahead_x(ez) - ez)
        keep = index > 0
        return (
            jnp.where(keep, hx - DT * curl_x, 0.0),
            jnp.where(keep, hy - DT * curl_y, 0.0),
        )

    def new_e(e, p, j, out, z, hn, hn_dn, step, strength):
        hx, hy, hz = hn
        hx_dn, hy_dn = hn_dn
        curl = (
            hz - behind_y(hz) - (hy - hy_dn),
            hx - hx_dn - (hz - behind_x(hz)),
            hy - behind_x(hy) - (hx - behind_y(hx)),
        )
        for c in range(3):
            j_next = (KEEP * j[c, z] + DT * (strength * e[c, z] - p[c, z])) * SHRINK
            out[c, z] = e[c, z] + step * (curl[c] - j_next)

    runs = ((ef, hf, pf, jf, hf_o, ef_o, 0), (ea, ha, pa, ja, ha_o, ea_o, 2))
    prev = [lower_h(ef, 0), lower_h(ea, 5)]
    for z in range(depth):
        density = rho[z]
        step = DT / (1.0 + EPS_RANGE * density)
        strength = STRENGTH_BASE + STRENGTH_RANGE * density
        for r, (e, h, p, j, h_out, e_out, up) in enumerate(runs):
            if z + 1 < depth:
                ex_up, ey_up = e[0, z + 1], e[1, z + 1]
            else:
                ex_up, ey_up = upper[up], upper[up + 1]
            hn = new_h(e, h, z, ex_up, ey_up)
            for c in range(3):
                h_out[c, z] = hn[c]
            new_e(e, p, j, e_out, z, hn, prev[r], step, strength)
            prev[r] = (hn[0], hn[1])

    plane = width_x * width_y
    tile_row = lax.broadcasted_iota(jnp.int32, (8, width_y), 0)
    tile_lane = lax.broadcasted_iota(jnp.int32, (8, width_y), 1)

    def add_at(cell, out, value_of):
        zz, x, y = split_cell(cell, width_x, width_y)
        local = zz - index * depth
        x0 = pl.multiple_of(x - lax.bitwise_and(x, 7), 8)

        @pl.when((local >= 0) & (local < depth))
        def _():
            rows = pl.ds(x0, 8)
            hit = (tile_row == x - x0) & (tile_lane == y)
            step = DT / (1.0 + EPS_RANGE * rho[local, rows, :])
            for c in range(3):
                held = out[c, local, rows, :]
                out[c, local, rows, :] = held + jnp.where(hit, step * value_of(c, local, rows), 0.0)

    for s in range(src.shape[0]):
        add_at(src[s], ef_o, lambda c, local, rows, s=s: amp[s, c])
    for m in range(mon.shape[0]):
        add_at(mon[m], ea_o, lambda c, local, rows: ef[c, local, rows, :])

    for g in range(slab):
        ret_o[g] = jnp.zeros((width_x, width_y), jnp.float32)
    for z in range(depth):
        total = None
        for c in range(3):
            fwd = ef_o[c, z]
            term = ea_o[c, z] * (fwd - ef[c, z] + GAIN_FIELD * fwd)
            total = term if total is None else total + term
        p = index * depth + z - start

        @pl.when((p >= 0) & (p < slab))
        def _():
            ret_o[jnp.clip(p, 0, slab - 1)] = total


def fields(e_forward, h_forward, p_forward, j_forward, e_adjoint, h_adjoint, p_adjoint, j_adjoint,
           arrived, upper, below, source_cell, monitor_cell, source_amp, slab_start):
    shape = e_forward.shape
    depth = shape[1]
    field = jax.ShapeDtypeStruct(shape, jnp.float32)
    vmem = pl.BlockSpec(memory_space=pltpu.VMEM)
    smem = pl.BlockSpec(memory_space=pltpu.SMEM)
    cells = shape[1] * shape[2] * shape[3]
    return pl.pallas_call(
        field_kernel,
        out_shape=(field, field, field, field, jax.ShapeDtypeStruct(arrived.shape, jnp.float32)),
        in_specs=[vmem] * 11 + [smem] * 4,
        out_specs=(vmem,) * 5,
        scratch_shapes=[pltpu.VMEM(shape[1:], jnp.float32)],
        compiler_params=pltpu.CompilerParams(vmem_limit_bytes=48 * 1024 * 1024),
        cost_estimate=pl.CostEstimate(
            flops=200 * cells, bytes_accessed=4 * cells * 40, transcendentals=0
        ),
    )(e_forward, h_forward, p_forward, j_forward, e_adjoint, h_adjoint, p_adjoint, j_adjoint,
      arrived, upper, below, source_cell, monitor_cell, source_amp, slab_start)


def body(
    e_forward,
    h_forward,
    p_forward,
    j_forward,
    e_adjoint,
    h_adjoint,
    p_adjoint,
    j_adjoint,
    design,
    source_amp,
    source_cell,
    monitor_cell,
    slab_start,
    radius,
):
    count = lax.axis_size("gx")
    index = lax.axis_index("gx")
    depth, width_x, width_y = (e_forward.shape[1], e_forward.shape[2], e_forward.shape[3])
    start = slab_start[0]
    wx = band_matrix(width_x, radius[0])
    wy = band_matrix(width_y, radius[0])
    upper = passed_along(jnp.concatenate([e_forward[0:2, 0], e_adjoint[0:2, 0]], 0), "gx", -1)
    below = passed_along(
        jnp.concatenate(
            [h_forward[0:2, -1], e_forward[:, -1], h_adjoint[0:2, -1], e_adjoint[:, -1]], 0
        ),
        "gx",
        1,
    )
    owned = smooth(wx, wy, design)
    slots = jnp.broadcast_to(owned, (count,) + owned.shape[1:])
    arrived = lax.all_to_all(slots, "gx", split_axis=0, concat_axis=0, tiled=True)
    ef, hf, ea, ha, returned = fields(
        e_forward, h_forward, p_forward, j_forward, e_adjoint, h_adjoint, p_adjoint, j_adjoint,
        arrived, upper, below, source_cell, monitor_cell, source_amp, slab_start,
    )
    arrived_back = lax.all_to_all(returned, "gx", split_axis=0, concat_axis=0, tiled=True)
    inner = jnp.einsum("ax,jab->xb", wx, arrived_back, precision=HIGH)
    design_grad = jnp.einsum("xb,by->xy", inner, wy, precision=HIGH)[None]
    return (ef, hf, ea, ha, design_grad)


def solution(mesh):
    return jax.shard_map(
        body,
        mesh=mesh,
        in_specs=(
            P(None, ("grp", "gx"), None, None),
            P(None, ("grp", "gx"), None, None),
            P(None, ("grp", "gx"), None, None),
            P(None, ("grp", "gx"), None, None),
            P(None, ("grp", "gx"), None, None),
            P(None, ("grp", "gx"), None, None),
            P(None, ("grp", "gx"), None, None),
            P(None, ("grp", "gx"), None, None),
            P(("grp", "gx"), None, None),
            P("grp", None),
            P("grp"),
            P("grp"),
            P("grp"),
            P("grp"),
        ),
        out_specs=(
            P(None, ("grp", "gx"), None, None),
            P(None, ("grp", "gx"), None, None),
            P(None, ("grp", "gx"), None, None),
            P(None, ("grp", "gx"), None, None),
            P(("grp", "gx"), None, None),
        ),
        check_vma=False,
    )
```

```python
import functools

import jax
import jax.numpy as jnp
from jax import lax
from jax.experimental import pallas as pl
from jax.experimental.pallas import tpu as pltpu
from jax.sharding import PartitionSpec as P

DT = 0.5
EPS_RANGE = 10.0
STRENGTH_BASE = 0.5
STRENGTH_RANGE = 3.0
DAMPING = 0.2
GAIN_FIELD = 0.25
HIGH = lax.Precision.HIGHEST
KEEP = 1.0 - DAMPING * DT / 2.0
LOSS = 1.0 + DAMPING * DT / 2.0
SHRINK = 1.0 / LOSS


def passed_along(block, axis, distance):
    devices = range(lax.axis_size(axis))
    route = [(i - distance, i) for i in devices if i - distance in devices]
    return lax.ppermute(block, axis, route)


def band_matrix(count, radius):
    rows = jnp.arange(count, dtype=jnp.int32)
    dist = jnp.abs(rows[:, None] - rows[None, :])
    weights = jnp.maximum(radius + 1 - dist, 0).astype(jnp.float32)
    return weights / jnp.sum(weights, axis=1, keepdims=True)


def smooth(wx, wy, planes):
    inner = jnp.einsum("ax,zxy->zay", wx, planes, precision=HIGH)
    return jnp.einsum("zay,by->zab", inner, wy, precision=HIGH)


def smooth_adjoint(wx, wy, planes):
    inner = jnp.einsum("ax,zab->zxb", wx, planes, precision=HIGH)
    return jnp.einsum("zxb,by->zxy", inner, wy, precision=HIGH)


def split_cell(cell, width_x, width_y):
    plane = width_x * width_y
    if plane & (plane - 1) == 0 and width_y & (width_y - 1) == 0:
        zz = lax.shift_right_arithmetic(cell, plane.bit_length() - 1)
        rest = lax.bitwise_and(cell, plane - 1)
        x = lax.shift_right_arithmetic(rest, width_y.bit_length() - 1)
        return zz, x, lax.bitwise_and(rest, width_y - 1)
    zz = cell // plane
    rest = cell - zz * plane
    x = rest // width_y
    return zz, x, rest - x * width_y


def field_kernel(
    ef, hf, pf, jf, ea, ha, pa, ja, arrived, upper, below, src, mon, amp, first,
    ef_o, hf_o, ea_o, ha_o, ret_o, rho,
):
    depth, width_x, width_y = rho.shape
    slab = arrived.shape[0]
    index = lax.axis_index("gx")
    start = first[0]
    for z in range(depth):
        p = index * depth + z - start
        inside = (p >= 0) & (p < slab)
        rho[z] = jnp.where(inside, arrived[jnp.clip(p, 0, slab - 1)], 0.0)
    row = lax.broadcasted_iota(jnp.int32, (width_x, width_y), 0)
    lane = lax.broadcasted_iota(jnp.int32, (width_x, width_y), 1)

    def ahead_y(f):
        return jnp.where(lane == width_y - 1, 0.0, pltpu.roll(f, width_y - 1, 1))

    def ahead_x(f):
        return jnp.where(row == width_x - 1, 0.0, pltpu.roll(f, width_x - 1, 0))

    def behind_y(f):
        return jnp.where(lane == 0, 0.0, pltpu.roll(f, 1, 1))

    def behind_x(f):
        return jnp.where(row == 0, 0.0, pltpu.roll(f, 1, 0))

    def new_h(e, h, z, ex_up, ey_up):
        ex, ey, ez = e[0, z], e[1, z], e[2, z]
        curl_x = ahead_y(ez) - ez - (ey_up - ey)
        curl_y = ex_up - ex - (ahead_x(ez) - ez)
        curl_z = ahead_x(ey) - ey - (ahead_y(ex) - ex)
        return (h[0, z] - DT * curl_x, h[1, z] - DT * curl_y, h[2, z] - DT * curl_z)

    def lower_h(e, base):
        hx, hy, ex, ey, ez = (below[base + i] for i in range(5))
        curl_x = ahead_y(ez) - ez - (e[1, 0] - ey)
        curl_y = e[0, 0] - ex - (ahead_x(ez) - ez)
        keep = index > 0
        return (
            jnp.where(keep, hx - DT * curl_x, 0.0),
            jnp.where(keep, hy - DT * curl_y, 0.0),
        )

    def new_e(e, p, j, out, z, hn, hn_dn, step, strength):
        hx, hy, hz = hn
        hx_dn, hy_dn = hn_dn
        curl = (
            hz - behind_y(hz) - (hy - hy_dn),
            hx - hx_dn - (hz - behind_x(hz)),
            hy - behind_x(hy) - (hx - behind_y(hx)),
        )
        for c in range(3):
            j_next = (KEEP * j[c, z] + DT * (strength * e[c, z] - p[c, z])) * SHRINK
            out[c, z] = e[c, z] + step * (curl[c] - j_next)

    runs = ((ef, hf, pf, jf, hf_o, ef_o, 0), (ea, ha, pa, ja, ha_o, ea_o, 2))
    prev = [lower_h(ef, 0), lower_h(ea, 5)]
    for z in range(depth):
        density = rho[z]
        step = DT / (1.0 + EPS_RANGE * density)
        strength = STRENGTH_BASE + STRENGTH_RANGE * density
        for r, (e, h, p, j, h_out, e_out, up) in enumerate(runs):
            if z + 1 < depth:
                ex_up, ey_up = e[0, z + 1], e[1, z + 1]
            else:
                ex_up, ey_up = upper[up], upper[up + 1]
            hn = new_h(e, h, z, ex_up, ey_up)
            for c in range(3):
                h_out[c, z] = hn[c]
            new_e(e, p, j, e_out, z, hn, prev[r], step, strength)
            prev[r] = (hn[0], hn[1])

    plane = width_x * width_y
    tile_row = lax.broadcasted_iota(jnp.int32, (8, width_y), 0)
    tile_lane = lax.broadcasted_iota(jnp.int32, (8, width_y), 1)

    def add_at(cell, out, value_of):
        zz, x, y = split_cell(cell, width_x, width_y)
        local = zz - index * depth
        x0 = pl.multiple_of(x - lax.bitwise_and(x, 7), 8)

        @pl.when((local >= 0) & (local < depth))
        def _():
            rows = pl.ds(x0, 8)
            hit = (tile_row == x - x0) & (tile_lane == y)
            step = DT / (1.0 + EPS_RANGE * rho[local, rows, :])
            for c in range(3):
                held = out[c, local, rows, :]
                out[c, local, rows, :] = held + jnp.where(hit, step * value_of(c, local, rows), 0.0)

    for s in range(src.shape[0]):
        add_at(src[s], ef_o, lambda c, local, rows, s=s: amp[s, c])
    for m in range(mon.shape[0]):
        add_at(mon[m], ea_o, lambda c, local, rows: ef[c, local, rows, :])

    for g in range(slab):
        ret_o[g] = jnp.zeros((width_x, width_y), jnp.float32)
    for z in range(depth):
        total = None
        for c in range(3):
            fwd = ef_o[c, z]
            term = ea_o[c, z] * (fwd - ef[c, z] + GAIN_FIELD * fwd)
            total = term if total is None else total + term
        p = index * depth + z - start

        @pl.when((p >= 0) & (p < slab))
        def _():
            ret_o[jnp.clip(p, 0, slab - 1)] = total


def fields(e_forward, h_forward, p_forward, j_forward, e_adjoint, h_adjoint, p_adjoint, j_adjoint,
           arrived, upper, below, source_cell, monitor_cell, source_amp, slab_start):
    shape = e_forward.shape
    depth = shape[1]
    field = jax.ShapeDtypeStruct(shape, jnp.float32)
    vmem = pl.BlockSpec(memory_space=pltpu.VMEM)
    smem = pl.BlockSpec(memory_space=pltpu.SMEM)
    cells = shape[1] * shape[2] * shape[3]
    return pl.pallas_call(
        field_kernel,
        out_shape=(field, field, field, field, jax.ShapeDtypeStruct(arrived.shape, jnp.float32)),
        in_specs=[vmem] * 11 + [smem] * 4,
        out_specs=(vmem,) * 5,
        scratch_shapes=[pltpu.VMEM(shape[1:], jnp.float32)],
        compiler_params=pltpu.CompilerParams(vmem_limit_bytes=50 * 1024 * 1024),
        cost_estimate=pl.CostEstimate(
            flops=200 * cells, bytes_accessed=4 * cells * 40, transcendentals=0
        ),
    )(e_forward, h_forward, p_forward, j_forward, e_adjoint, h_adjoint, p_adjoint, j_adjoint,
      arrived, upper, below, source_cell, monitor_cell, source_amp, slab_start)


def body(
    e_forward,
    h_forward,
    p_forward,
    j_forward,
    e_adjoint,
    h_adjoint,
    p_adjoint,
    j_adjoint,
    design,
    source_amp,
    source_cell,
    monitor_cell,
    slab_start,
    radius,
):
    count = lax.axis_size("gx")
    index = lax.axis_index("gx")
    depth, width_x, width_y = (e_forward.shape[1], e_forward.shape[2], e_forward.shape[3])
    start = slab_start[0]
    wx = band_matrix(width_x, radius[0])
    wy = band_matrix(width_y, radius[0])
    upper = passed_along(jnp.concatenate([e_forward[0:2, 0], e_adjoint[0:2, 0]], 0), "gx", -1)
    below = passed_along(
        jnp.concatenate(
            [h_forward[0:2, -1], e_forward[:, -1], h_adjoint[0:2, -1], e_adjoint[:, -1]], 0
        ),
        "gx",
        1,
    )
    owned = smooth(wx, wy, design)
    slots = jnp.broadcast_to(owned, (count,) + owned.shape[1:])
    arrived = lax.all_to_all(slots, "gx", split_axis=0, concat_axis=0, tiled=True)
    ef, hf, ea, ha, returned = fields(
        e_forward, h_forward, p_forward, j_forward, e_adjoint, h_adjoint, p_adjoint, j_adjoint,
        arrived, upper, below, source_cell, monitor_cell, source_amp, slab_start,
    )
    arrived_back = lax.all_to_all(returned, "gx", split_axis=0, concat_axis=0, tiled=True)
    inner = jnp.einsum("ax,jab->xb", wx, arrived_back, precision=HIGH)
    design_grad = jnp.einsum("xb,by->xy", inner, wy, precision=HIGH)[None]
    return (ef, hf, ea, ha, design_grad)


def solution(mesh):
    return jax.shard_map(
        body,
        mesh=mesh,
        in_specs=(
            P(None, ("grp", "gx"), None, None),
            P(None, ("grp", "gx"), None, None),
            P(None, ("grp", "gx"), None, None),
            P(None, ("grp", "gx"), None, None),
            P(None, ("grp", "gx"), None, None),
            P(None, ("grp", "gx"), None, None),
            P(None, ("grp", "gx"), None, None),
            P(None, ("grp", "gx"), None, None),
            P(("grp", "gx"), None, None),
            P("grp", None),
            P("grp"),
            P("grp"),
            P("grp"),
            P("grp"),
        ),
        out_specs=(
            P(None, ("grp", "gx"), None, None),
            P(None, ("grp", "gx"), None, None),
            P(None, ("grp", "gx"), None, None),
            P(None, ("grp", "gx"), None, None),
            P(("grp", "gx"), None, None),
        ),
        check_vma=False,
    )
```

```python
import functools

import jax
import jax.numpy as jnp
from jax import lax
from jax.experimental import pallas as pl
from jax.experimental.pallas import tpu as pltpu
from jax.sharding import PartitionSpec as P

DT = 0.5
EPS_RANGE = 10.0
STRENGTH_BASE = 0.5
STRENGTH_RANGE = 3.0
DAMPING = 0.2
GAIN_FIELD = 0.25
HIGH = lax.Precision.HIGHEST
KEEP = 1.0 - DAMPING * DT / 2.0
LOSS = 1.0 + DAMPING * DT / 2.0
SHRINK = 1.0 / LOSS


def passed_along(block, axis, distance):
    devices = range(lax.axis_size(axis))
    route = [(i - distance, i) for i in devices if i - distance in devices]
    return lax.ppermute(block, axis, route)


def band_matrix(count, radius):
    rows = jnp.arange(count, dtype=jnp.int32)
    dist = jnp.abs(rows[:, None] - rows[None, :])
    weights = jnp.maximum(radius + 1 - dist, 0).astype(jnp.float32)
    return weights / jnp.sum(weights, axis=1, keepdims=True)


def smooth(wx, wy, planes):
    inner = jnp.einsum("ax,zxy->zay", wx, planes, precision=HIGH)
    return jnp.einsum("zay,by->zab", inner, wy, precision=HIGH)


def smooth_adjoint(wx, wy, planes):
    inner = jnp.einsum("ax,zab->zxb", wx, planes, precision=HIGH)
    return jnp.einsum("zxb,by->zxy", inner, wy, precision=HIGH)


def split_cell(cell, width_x, width_y):
    plane = width_x * width_y
    if plane & (plane - 1) == 0 and width_y & (width_y - 1) == 0:
        zz = lax.shift_right_arithmetic(cell, plane.bit_length() - 1)
        rest = lax.bitwise_and(cell, plane - 1)
        x = lax.shift_right_arithmetic(rest, width_y.bit_length() - 1)
        return zz, x, lax.bitwise_and(rest, width_y - 1)
    zz = cell // plane
    rest = cell - zz * plane
    x = rest // width_y
    return zz, x, rest - x * width_y


def field_kernel(
    ef_h, hf_h, pf_h, jf_h, ea_h, ha_h, pa_h, ja_h, arrived, upper, below, src, mon, amp, first,
    ef_oh, hf_oh, ea_oh, ha_oh, ret_o,
    ins, outs, rho, in_sem, out_sem,
):
    depth, width_x, width_y = rho.shape
    slab = arrived.shape[0]
    index = lax.axis_index("gx")
    start = first[0]
    sources = (ef_h, hf_h, pf_h, jf_h, ea_h, ha_h, pa_h, ja_h)
    targets = (ef_oh, hf_oh, ea_oh, ha_oh)

    def fetch(a, z):
        return pltpu.make_async_copy(
            sources[a].at[:, pl.ds(z, 1)], ins.at[a, :, pl.ds(z, 1)], in_sem.at[a, z]
        )

    def store(a, z):
        return pltpu.make_async_copy(
            outs.at[a, :, pl.ds(z, 1)], targets[a].at[:, pl.ds(z, 1)], out_sem.at[a, z]
        )

    for z in range(depth):
        for a in range(8):
            fetch(a, z).start()

    for z in range(depth):
        p = index * depth + z - start
        inside = (p >= 0) & (p < slab)
        rho[z] = jnp.where(inside, arrived[jnp.clip(p, 0, slab - 1)], 0.0)
    for g in range(slab):
        ret_o[g] = jnp.zeros((width_x, width_y), jnp.float32)

    row = lax.broadcasted_iota(jnp.int32, (width_x, width_y), 0)
    lane = lax.broadcasted_iota(jnp.int32, (width_x, width_y), 1)

    def ahead_y(f):
        return jnp.where(lane == width_y - 1, 0.0, pltpu.roll(f, width_y - 1, 1))

    def ahead_x(f):
        return jnp.where(row == width_x - 1, 0.0, pltpu.roll(f, width_x - 1, 0))

    def behind_y(f):
        return jnp.where(lane == 0, 0.0, pltpu.roll(f, 1, 1))

    def behind_x(f):
        return jnp.where(row == 0, 0.0, pltpu.roll(f, 1, 0))

    keep = index > 0
    prev = []
    for r in range(2):
        fetch(4 * r, 0).wait()
        fetch(4 * r + 1, 0).wait()
        fetch(4 * r + 2, 0).wait()
        fetch(4 * r + 3, 0).wait()
        hx, hy, ex, ey, ez = (below[5 * r + i] for i in range(5))
        e = ins.at[4 * r]
        curl_x = ahead_y(ez) - ez - (e[1, 0] - ey)
        curl_y = e[0, 0] - ex - (ahead_x(ez) - ez)
        prev.append((jnp.where(keep, hx - DT * curl_x, 0.0), jnp.where(keep, hy - DT * curl_y, 0.0)))

    for z in range(depth):
        if z + 1 < depth:
            for a in range(8):
                fetch(a, z + 1).wait()
        density = rho[z]
        step = DT / (1.0 + EPS_RANGE * density)
        strength = STRENGTH_BASE + STRENGTH_RANGE * density
        for r in range(2):
            e, h, p, j = (ins.at[4 * r + i] for i in range(4))
            if z + 1 < depth:
                ex_up, ey_up = e[0, z + 1], e[1, z + 1]
            else:
                ex_up, ey_up = upper[2 * r], upper[2 * r + 1]
            ex, ey, ez = e[0, z], e[1, z], e[2, z]
            hx = h[0, z] - DT * (ahead_y(ez) - ez - (ey_up - ey))
            hy = h[1, z] - DT * (ex_up - ex - (ahead_x(ez) - ez))
            hz = h[2, z] - DT * (ahead_x(ey) - ey - (ahead_y(ex) - ex))
            outs[2 * r + 1, 0, z] = hx
            outs[2 * r + 1, 1, z] = hy
            outs[2 * r + 1, 2, z] = hz
            store(2 * r + 1, z).start()
            hx_dn, hy_dn = prev[r]
            curl = (
                hz - behind_y(hz) - (hy - hy_dn),
                hx - hx_dn - (hz - behind_x(hz)),
                hy - behind_x(hy) - (hx - behind_y(hx)),
            )
            for c in range(3):
                j_next = (KEEP * j[c, z] + DT * (strength * e[c, z] - p[c, z])) * SHRINK
                outs[2 * r, c, z] = e[c, z] + step * (curl[c] - j_next)
            prev[r] = (hx, hy)

    tile_row = lax.broadcasted_iota(jnp.int32, (8, width_y), 0)
    tile_lane = lax.broadcasted_iota(jnp.int32, (8, width_y), 1)

    def add_at(cell, out, value_of):
        zz, x, y = split_cell(cell, width_x, width_y)
        local = zz - index * depth
        x0 = pl.multiple_of(x - lax.bitwise_and(x, 7), 8)

        @pl.when((local >= 0) & (local < depth))
        def _():
            rows = pl.ds(x0, 8)
            hit = (tile_row == x - x0) & (tile_lane == y)
            gain = DT / (1.0 + EPS_RANGE * rho[local, rows, :])
            for c in range(3):
                held = outs[out, c, local, rows, :]
                outs[out, c, local, rows, :] = held + jnp.where(hit, gain * value_of(c, local, rows), 0.0)

    for s in range(src.shape[0]):
        add_at(src[s], 0, lambda c, local, rows, s=s: amp[s, c])
    for m in range(mon.shape[0]):
        add_at(mon[m], 2, lambda c, local, rows: ins[0, c, local, rows, :])
    for z in range(depth):
        store(0, z).start()
        store(2, z).start()

    for z in range(depth):
        total = None
        for c in range(3):
            fwd = outs[0, c, z]
            term = outs[2, c, z] * (fwd - ins[0, c, z] + GAIN_FIELD * fwd)
            total = term if total is None else total + term
        p = index * depth + z - start

        @pl.when((p >= 0) & (p < slab))
        def _():
            ret_o[jnp.clip(p, 0, slab - 1)] = total

    for z in range(depth):
        for a in range(4):
            store(a, z).wait()


def fields(e_forward, h_forward, p_forward, j_forward, e_adjoint, h_adjoint, p_adjoint, j_adjoint,
           arrived, upper, below, source_cell, monitor_cell, source_amp, slab_start):
    shape = e_forward.shape
    depth = shape[1]
    field = jax.ShapeDtypeStruct(shape, jnp.float32)
    hbm = pl.BlockSpec(memory_space=pl.ANY)
    vmem = pl.BlockSpec(memory_space=pltpu.VMEM)
    smem = pl.BlockSpec(memory_space=pltpu.SMEM)
    cells = shape[1] * shape[2] * shape[3]
    return pl.pallas_call(
        field_kernel,
        out_shape=(field, field, field, field, jax.ShapeDtypeStruct(arrived.shape, jnp.float32)),
        in_specs=[hbm] * 8 + [vmem] * 3 + [smem] * 4,
        out_specs=(hbm,) * 4 + (vmem,),
        scratch_shapes=[
            pltpu.VMEM((8,) + shape, jnp.float32),
            pltpu.VMEM((4,) + shape, jnp.float32),
            pltpu.VMEM(shape[1:], jnp.float32),
            pltpu.SemaphoreType.DMA((8, depth)),
            pltpu.SemaphoreType.DMA((4, depth)),
        ],
        compiler_params=pltpu.CompilerParams(vmem_limit_bytes=50 * 1024 * 1024),
        cost_estimate=pl.CostEstimate(
            flops=200 * cells, bytes_accessed=4 * cells * 40, transcendentals=0
        ),
    )(e_forward, h_forward, p_forward, j_forward, e_adjoint, h_adjoint, p_adjoint, j_adjoint,
      arrived, upper, below, source_cell, monitor_cell, source_amp, slab_start)


def body(
    e_forward,
    h_forward,
    p_forward,
    j_forward,
    e_adjoint,
    h_adjoint,
    p_adjoint,
    j_adjoint,
    design,
    source_amp,
    source_cell,
    monitor_cell,
    slab_start,
    radius,
):
    count = lax.axis_size("gx")
    index = lax.axis_index("gx")
    depth, width_x, width_y = (e_forward.shape[1], e_forward.shape[2], e_forward.shape[3])
    start = slab_start[0]
    wx = band_matrix(width_x, radius[0])
    wy = band_matrix(width_y, radius[0])
    upper = passed_along(jnp.concatenate([e_forward[0:2, 0], e_adjoint[0:2, 0]], 0), "gx", -1)
    below = passed_along(
        jnp.concatenate(
            [h_forward[0:2, -1], e_forward[:, -1], h_adjoint[0:2, -1], e_adjoint[:, -1]], 0
        ),
        "gx",
        1,
    )
    owned = smooth(wx, wy, design)
    slots = jnp.broadcast_to(owned, (count,) + owned.shape[1:])
    arrived = lax.all_to_all(slots, "gx", split_axis=0, concat_axis=0, tiled=True)
    ef, hf, ea, ha, returned = fields(
        e_forward, h_forward, p_forward, j_forward, e_adjoint, h_adjoint, p_adjoint, j_adjoint,
        arrived, upper, below, source_cell, monitor_cell, source_amp, slab_start,
    )
    arrived_back = lax.all_to_all(returned, "gx", split_axis=0, concat_axis=0, tiled=True)
    inner = jnp.einsum("ax,jab->xb", wx, arrived_back, precision=HIGH)
    design_grad = jnp.einsum("xb,by->xy", inner, wy, precision=HIGH)[None]
    return (ef, hf, ea, ha, design_grad)


def solution(mesh):
    return jax.shard_map(
        body,
        mesh=mesh,
        in_specs=(
            P(None, ("grp", "gx"), None, None),
            P(None, ("grp", "gx"), None, None),
            P(None, ("grp", "gx"), None, None),
            P(None, ("grp", "gx"), None, None),
            P(None, ("grp", "gx"), None, None),
            P(None, ("grp", "gx"), None, None),
            P(None, ("grp", "gx"), None, None),
            P(None, ("grp", "gx"), None, None),
            P(("grp", "gx"), None, None),
            P("grp", None),
            P("grp"),
            P("grp"),
            P("grp"),
            P("grp"),
        ),
        out_specs=(
            P(None, ("grp", "gx"), None, None),
            P(None, ("grp", "gx"), None, None),
            P(None, ("grp", "gx"), None, None),
            P(None, ("grp", "gx"), None, None),
            P(("grp", "gx"), None, None),
        ),
        check_vma=False,
    )
```

```python
import functools

import jax
import jax.numpy as jnp
from jax import lax
from jax.experimental import pallas as pl
from jax.experimental.pallas import tpu as pltpu
from jax.sharding import PartitionSpec as P

DT = 0.5
EPS_RANGE = 10.0
STRENGTH_BASE = 0.5
STRENGTH_RANGE = 3.0
DAMPING = 0.2
GAIN_FIELD = 0.25
HIGH = lax.Precision.HIGHEST
KEEP = 1.0 - DAMPING * DT / 2.0
LOSS = 1.0 + DAMPING * DT / 2.0
SHRINK = 1.0 / LOSS


def passed_along(block, axis, distance):
    devices = range(lax.axis_size(axis))
    route = [(i - distance, i) for i in devices if i - distance in devices]
    return lax.ppermute(block, axis, route)


def band_matrix(count, radius):
    rows = jnp.arange(count, dtype=jnp.int32)
    dist = jnp.abs(rows[:, None] - rows[None, :])
    weights = jnp.maximum(radius + 1 - dist, 0).astype(jnp.float32)
    return weights / jnp.sum(weights, axis=1, keepdims=True)


def smooth(wx, wy, planes):
    inner = jnp.einsum("ax,zxy->zay", wx, planes, precision=HIGH)
    return jnp.einsum("zay,by->zab", inner, wy, precision=HIGH)


def smooth_adjoint(wx, wy, planes):
    inner = jnp.einsum("ax,zab->zxb", wx, planes, precision=HIGH)
    return jnp.einsum("zxb,by->zxy", inner, wy, precision=HIGH)


def split_cell(cell, width_x, width_y):
    plane = width_x * width_y
    if plane & (plane - 1) == 0 and width_y & (width_y - 1) == 0:
        zz = lax.shift_right_arithmetic(cell, plane.bit_length() - 1)
        rest = lax.bitwise_and(cell, plane - 1)
        x = lax.shift_right_arithmetic(rest, width_y.bit_length() - 1)
        return zz, x, lax.bitwise_and(rest, width_y - 1)
    zz = cell // plane
    rest = cell - zz * plane
    x = rest // width_y
    return zz, x, rest - x * width_y


def shifts(width_x, width_y):
    row = lax.broadcasted_iota(jnp.int32, (width_x, width_y), 0)
    lane = lax.broadcasted_iota(jnp.int32, (width_x, width_y), 1)

    def ahead_y(f):
        return jnp.where(lane == width_y - 1, 0.0, pltpu.roll(f, width_y - 1, 1))

    def ahead_x(f):
        return jnp.where(row == width_x - 1, 0.0, pltpu.roll(f, width_x - 1, 0))

    def behind_y(f):
        return jnp.where(lane == 0, 0.0, pltpu.roll(f, 1, 1))

    def behind_x(f):
        return jnp.where(row == 0, 0.0, pltpu.roll(f, 1, 0))

    return ahead_y, ahead_x, behind_y, behind_x


def h_kernel(ef, hf, ea, ha, upper, below, hf_o, ha_o, lower):
    _, depth, width_x, width_y = ef.shape
    ahead_y, ahead_x, _, _ = shifts(width_x, width_y)
    keep = lax.axis_index("gx") > 0
    for r, (e, h, h_out) in enumerate(((ef, hf, hf_o), (ea, ha, ha_o))):
        hx, hy, ex, ey, ez = (below[5 * r + i] for i in range(5))
        curl_x = ahead_y(ez) - ez - (e[1, 0] - ey)
        curl_y = e[0, 0] - ex - (ahead_x(ez) - ez)
        lower[2 * r] = jnp.where(keep, hx - DT * curl_x, 0.0)
        lower[2 * r + 1] = jnp.where(keep, hy - DT * curl_y, 0.0)
        for z in range(depth):
            if z + 1 < depth:
                ex_up, ey_up = e[0, z + 1], e[1, z + 1]
            else:
                ex_up, ey_up = upper[2 * r], upper[2 * r + 1]
            ex, ey, ez = e[0, z], e[1, z], e[2, z]
            h_out[0, z] = h[0, z] - DT * (ahead_y(ez) - ez - (ey_up - ey))
            h_out[1, z] = h[1, z] - DT * (ex_up - ex - (ahead_x(ez) - ez))
            h_out[2, z] = h[2, z] - DT * (ahead_x(ey) - ey - (ahead_y(ex) - ex))


def e_kernel(
    ef, pf, jf, ea, pa, ja, hfn, han, lower, arrived, src, mon, amp, first,
    ef_o, ea_o, ret_o, rho,
):
    depth, width_x, width_y = rho.shape
    slab = arrived.shape[0]
    index = lax.axis_index("gx")
    start = first[0]
    for z in range(depth):
        p = index * depth + z - start
        inside = (p >= 0) & (p < slab)
        rho[z] = jnp.where(inside, arrived[jnp.clip(p, 0, slab - 1)], 0.0)
    _, _, behind_y, behind_x = shifts(width_x, width_y)

    runs = ((ef, pf, jf, hfn, ef_o), (ea, pa, ja, han, ea_o))
    for z in range(depth):
        density = rho[z]
        step = DT / (1.0 + EPS_RANGE * density)
        strength = STRENGTH_BASE + STRENGTH_RANGE * density
        for r, (e, p, j, hn, e_out) in enumerate(runs):
            hx, hy, hz = hn[0, z], hn[1, z], hn[2, z]
            if z > 0:
                hx_dn, hy_dn = hn[0, z - 1], hn[1, z - 1]
            else:
                hx_dn, hy_dn = lower[2 * r], lower[2 * r + 1]
            curl = (
                hz - behind_y(hz) - (hy - hy_dn),
                hx - hx_dn - (hz - behind_x(hz)),
                hy - behind_x(hy) - (hx - behind_y(hx)),
            )
            for c in range(3):
                j_next = (KEEP * j[c, z] + DT * (strength * e[c, z] - p[c, z])) * SHRINK
                e_out[c, z] = e[c, z] + step * (curl[c] - j_next)

    plane = width_x * width_y
    tile_row = lax.broadcasted_iota(jnp.int32, (8, width_y), 0)
    tile_lane = lax.broadcasted_iota(jnp.int32, (8, width_y), 1)

    def add_at(cell, out, value_of):
        zz, x, y = split_cell(cell, width_x, width_y)
        local = zz - index * depth
        x0 = pl.multiple_of(x - lax.bitwise_and(x, 7), 8)

        @pl.when((local >= 0) & (local < depth))
        def _():
            rows = pl.ds(x0, 8)
            hit = (tile_row == x - x0) & (tile_lane == y)
            gain = DT / (1.0 + EPS_RANGE * rho[local, rows, :])
            for c in range(3):
                held = out[c, local, rows, :]
                out[c, local, rows, :] = held + jnp.where(hit, gain * value_of(c, local, rows), 0.0)

    for s in range(src.shape[0]):
        add_at(src[s], ef_o, lambda c, local, rows, s=s: amp[s, c])
    for m in range(mon.shape[0]):
        add_at(mon[m], ea_o, lambda c, local, rows: ef[c, local, rows, :])

    for g in range(slab):
        ret_o[g] = jnp.zeros((width_x, width_y), jnp.float32)
    for z in range(depth):
        total = None
        for c in range(3):
            fwd = ef_o[c, z]
            term = ea_o[c, z] * (fwd - ef[c, z] + GAIN_FIELD * fwd)
            total = term if total is None else total + term
        p = index * depth + z - start

        @pl.when((p >= 0) & (p < slab))
        def _():
            ret_o[jnp.clip(p, 0, slab - 1)] = total


def fields(e_forward, h_forward, p_forward, j_forward, e_adjoint, h_adjoint, p_adjoint, j_adjoint,
           arrived, upper, below, source_cell, monitor_cell, source_amp, slab_start):
    shape = e_forward.shape
    field = jax.ShapeDtypeStruct(shape, jnp.float32)
    vmem = pl.BlockSpec(memory_space=pltpu.VMEM)
    smem = pl.BlockSpec(memory_space=pltpu.SMEM)
    cells = shape[1] * shape[2] * shape[3]
    hf, ha, lower = pl.pallas_call(
        h_kernel,
        out_shape=(field, field, jax.ShapeDtypeStruct((4,) + shape[2:], jnp.float32)),
        in_specs=[vmem] * 6,
        out_specs=(vmem,) * 3,
        compiler_params=pltpu.CompilerParams(vmem_limit_bytes=12 * 1024 * 1024),
        cost_estimate=pl.CostEstimate(
            flops=60 * cells, bytes_accessed=4 * cells * 18, transcendentals=0
        ),
    )(e_forward, h_forward, e_adjoint, h_adjoint, upper, below)
    ef, ea, returned = pl.pallas_call(
        e_kernel,
        out_shape=(field, field, jax.ShapeDtypeStruct(arrived.shape, jnp.float32)),
        in_specs=[vmem] * 10 + [smem] * 4,
        out_specs=(vmem,) * 3,
        scratch_shapes=[pltpu.VMEM(shape[1:], jnp.float32)],
        compiler_params=pltpu.CompilerParams(vmem_limit_bytes=52 * 1024 * 1024),
        cost_estimate=pl.CostEstimate(
            flops=140 * cells, bytes_accessed=4 * cells * 30, transcendentals=0
        ),
    )(e_forward, p_forward, j_forward, e_adjoint, p_adjoint, j_adjoint, hf, ha, lower, arrived,
      source_cell, monitor_cell, source_amp, slab_start)
    return ef, hf, ea, ha, returned


def body(
    e_forward,
    h_forward,
    p_forward,
    j_forward,
    e_adjoint,
    h_adjoint,
    p_adjoint,
    j_adjoint,
    design,
    source_amp,
    source_cell,
    monitor_cell,
    slab_start,
    radius,
):
    count = lax.axis_size("gx")
    index = lax.axis_index("gx")
    depth, width_x, width_y = (e_forward.shape[1], e_forward.shape[2], e_forward.shape[3])
    start = slab_start[0]
    wx = band_matrix(width_x, radius[0])
    wy = band_matrix(width_y, radius[0])
    upper = passed_along(jnp.concatenate([e_forward[0:2, 0], e_adjoint[0:2, 0]], 0), "gx", -1)
    below = passed_along(
        jnp.concatenate(
            [h_forward[0:2, -1], e_forward[:, -1], h_adjoint[0:2, -1], e_adjoint[:, -1]], 0
        ),
        "gx",
        1,
    )
    owned = smooth(wx, wy, design)
    slots = jnp.broadcast_to(owned, (count,) + owned.shape[1:])
    arrived = lax.all_to_all(slots, "gx", split_axis=0, concat_axis=0, tiled=True)
    ef, hf, ea, ha, returned = fields(
        e_forward, h_forward, p_forward, j_forward, e_adjoint, h_adjoint, p_adjoint, j_adjoint,
        arrived, upper, below, source_cell, monitor_cell, source_amp, slab_start,
    )
    arrived_back = lax.all_to_all(returned, "gx", split_axis=0, concat_axis=0, tiled=True)
    inner = jnp.einsum("ax,jab->xb", wx, arrived_back, precision=HIGH)
    design_grad = jnp.einsum("xb,by->xy", inner, wy, precision=HIGH)[None]
    return (ef, hf, ea, ha, design_grad)


def solution(mesh):
    return jax.shard_map(
        body,
        mesh=mesh,
        in_specs=(
            P(None, ("grp", "gx"), None, None),
            P(None, ("grp", "gx"), None, None),
            P(None, ("grp", "gx"), None, None),
            P(None, ("grp", "gx"), None, None),
            P(None, ("grp", "gx"), None, None),
            P(None, ("grp", "gx"), None, None),
            P(None, ("grp", "gx"), None, None),
            P(None, ("grp", "gx"), None, None),
            P(("grp", "gx"), None, None),
            P("grp", None),
            P("grp"),
            P("grp"),
            P("grp"),
            P("grp"),
        ),
        out_specs=(
            P(None, ("grp", "gx"), None, None),
            P(None, ("grp", "gx"), None, None),
            P(None, ("grp", "gx"), None, None),
            P(None, ("grp", "gx"), None, None),
            P(("grp", "gx"), None, None),
        ),
        check_vma=False,
    )
```

```python
import functools

import jax
import jax.numpy as jnp
from jax import lax
from jax.experimental import pallas as pl
from jax.experimental.pallas import tpu as pltpu
from jax.sharding import PartitionSpec as P

DT = 0.5
EPS_RANGE = 10.0
STRENGTH_BASE = 0.5
STRENGTH_RANGE = 3.0
DAMPING = 0.2
GAIN_FIELD = 0.25
HIGH = lax.Precision.HIGHEST
KEEP = 1.0 - DAMPING * DT / 2.0
LOSS = 1.0 + DAMPING * DT / 2.0
SHRINK = 1.0 / LOSS


def passed_along(block, axis, distance):
    devices = range(lax.axis_size(axis))
    route = [(i - distance, i) for i in devices if i - distance in devices]
    return lax.ppermute(block, axis, route)


def band_matrix(count, radius):
    rows = jnp.arange(count, dtype=jnp.int32)
    dist = jnp.abs(rows[:, None] - rows[None, :])
    weights = jnp.maximum(radius + 1 - dist, 0).astype(jnp.float32)
    return weights / jnp.sum(weights, axis=1, keepdims=True)


def smooth(wx, wy, planes):
    inner = jnp.einsum("ax,zxy->zay", wx, planes, precision=HIGH)
    return jnp.einsum("zay,by->zab", inner, wy, precision=HIGH)


def smooth_adjoint(wx, wy, planes):
    inner = jnp.einsum("ax,zab->zxb", wx, planes, precision=HIGH)
    return jnp.einsum("zxb,by->zxy", inner, wy, precision=HIGH)


def split_cell(cell, width_x, width_y):
    plane = width_x * width_y
    if plane & (plane - 1) == 0 and width_y & (width_y - 1) == 0:
        zz = lax.shift_right_arithmetic(cell, plane.bit_length() - 1)
        rest = lax.bitwise_and(cell, plane - 1)
        x = lax.shift_right_arithmetic(rest, width_y.bit_length() - 1)
        return zz, x, lax.bitwise_and(rest, width_y - 1)
    zz = cell // plane
    rest = cell - zz * plane
    x = rest // width_y
    return zz, x, rest - x * width_y


def field_kernel(
    ef, hf, pf, jf, ea, ha, pa, ja, arrived, upper, below, src, mon, amp, first,
    ef_oh, hf_oh, ea_oh, ha_oh, ret_o, rho, outs, out_sem,
):
    depth, width_x, width_y = rho.shape
    ef_o, hf_o, ea_o, ha_o = (outs.at[a] for a in range(4))
    targets = (ef_oh, hf_oh, ea_oh, ha_oh)

    def store(a, z):
        return pltpu.make_async_copy(
            outs.at[a, :, pl.ds(z, 1)], targets[a].at[:, pl.ds(z, 1)], out_sem.at[a, z]
        )

    slab = arrived.shape[0]
    index = lax.axis_index("gx")
    start = first[0]
    for z in range(depth):
        p = index * depth + z - start
        inside = (p >= 0) & (p < slab)
        rho[z] = jnp.where(inside, arrived[jnp.clip(p, 0, slab - 1)], 0.0)
    row = lax.broadcasted_iota(jnp.int32, (width_x, width_y), 0)
    lane = lax.broadcasted_iota(jnp.int32, (width_x, width_y), 1)

    def ahead_y(f):
        return jnp.where(lane == width_y - 1, 0.0, pltpu.roll(f, width_y - 1, 1))

    def ahead_x(f):
        return jnp.where(row == width_x - 1, 0.0, pltpu.roll(f, width_x - 1, 0))

    def behind_y(f):
        return jnp.where(lane == 0, 0.0, pltpu.roll(f, 1, 1))

    def behind_x(f):
        return jnp.where(row == 0, 0.0, pltpu.roll(f, 1, 0))

    def new_h(e, h, z, ex_up, ey_up):
        ex, ey, ez = e[0, z], e[1, z], e[2, z]
        curl_x = ahead_y(ez) - ez - (ey_up - ey)
        curl_y = ex_up - ex - (ahead_x(ez) - ez)
        curl_z = ahead_x(ey) - ey - (ahead_y(ex) - ex)
        return (h[0, z] - DT * curl_x, h[1, z] - DT * curl_y, h[2, z] - DT * curl_z)

    def lower_h(e, base):
        hx, hy, ex, ey, ez = (below[base + i] for i in range(5))
        curl_x = ahead_y(ez) - ez - (e[1, 0] - ey)
        curl_y = e[0, 0] - ex - (ahead_x(ez) - ez)
        keep = index > 0
        return (
            jnp.where(keep, hx - DT * curl_x, 0.0),
            jnp.where(keep, hy - DT * curl_y, 0.0),
        )

    def new_e(e, p, j, out, z, hn, hn_dn, step, strength):
        hx, hy, hz = hn
        hx_dn, hy_dn = hn_dn
        curl = (
            hz - behind_y(hz) - (hy - hy_dn),
            hx - hx_dn - (hz - behind_x(hz)),
            hy - behind_x(hy) - (hx - behind_y(hx)),
        )
        for c in range(3):
            j_next = (KEEP * j[c, z] + DT * (strength * e[c, z] - p[c, z])) * SHRINK
            out[c, z] = e[c, z] + step * (curl[c] - j_next)

    runs = ((ef, hf, pf, jf, hf_o, ef_o, 0), (ea, ha, pa, ja, ha_o, ea_o, 2))
    prev = [lower_h(ef, 0), lower_h(ea, 5)]
    for z in range(depth):
        density = rho[z]
        step = DT / (1.0 + EPS_RANGE * density)
        strength = STRENGTH_BASE + STRENGTH_RANGE * density
        for r, (e, h, p, j, h_out, e_out, up) in enumerate(runs):
            if z + 1 < depth:
                ex_up, ey_up = e[0, z + 1], e[1, z + 1]
            else:
                ex_up, ey_up = upper[up], upper[up + 1]
            hn = new_h(e, h, z, ex_up, ey_up)
            for c in range(3):
                h_out[c, z] = hn[c]
            store(2 * r + 1, z).start()
            new_e(e, p, j, e_out, z, hn, prev[r], step, strength)
            prev[r] = (hn[0], hn[1])

    plane = width_x * width_y
    tile_row = lax.broadcasted_iota(jnp.int32, (8, width_y), 0)
    tile_lane = lax.broadcasted_iota(jnp.int32, (8, width_y), 1)

    def add_at(cell, out, value_of):
        zz, x, y = split_cell(cell, width_x, width_y)
        local = zz - index * depth
        x0 = pl.multiple_of(x - lax.bitwise_and(x, 7), 8)

        @pl.when((local >= 0) & (local < depth))
        def _():
            rows = pl.ds(x0, 8)
            hit = (tile_row == x - x0) & (tile_lane == y)
            step = DT / (1.0 + EPS_RANGE * rho[local, rows, :])
            for c in range(3):
                held = out[c, local, rows, :]
                out[c, local, rows, :] = held + jnp.where(hit, step * value_of(c, local, rows), 0.0)

    for s in range(src.shape[0]):
        add_at(src[s], ef_o, lambda c, local, rows, s=s: amp[s, c])
    for m in range(mon.shape[0]):
        add_at(mon[m], ea_o, lambda c, local, rows: ef[c, local, rows, :])

    for z in range(depth):
        store(0, z).start()
        store(2, z).start()
    for g in range(slab):
        ret_o[g] = jnp.zeros((width_x, width_y), jnp.float32)
    for z in range(depth):
        total = None
        for c in range(3):
            fwd = ef_o[c, z]
            term = ea_o[c, z] * (fwd - ef[c, z] + GAIN_FIELD * fwd)
            total = term if total is None else total + term
        p = index * depth + z - start

        @pl.when((p >= 0) & (p < slab))
        def _():
            ret_o[jnp.clip(p, 0, slab - 1)] = total

    for z in range(depth):
        for a in range(4):
            store(a, z).wait()


def fields(e_forward, h_forward, p_forward, j_forward, e_adjoint, h_adjoint, p_adjoint, j_adjoint,
           arrived, upper, below, source_cell, monitor_cell, source_amp, slab_start):
    shape = e_forward.shape
    depth = shape[1]
    field = jax.ShapeDtypeStruct(shape, jnp.float32)
    vmem = pl.BlockSpec(memory_space=pltpu.VMEM)
    smem = pl.BlockSpec(memory_space=pltpu.SMEM)
    cells = shape[1] * shape[2] * shape[3]
    return pl.pallas_call(
        field_kernel,
        out_shape=(field, field, field, field, jax.ShapeDtypeStruct(arrived.shape, jnp.float32)),
        in_specs=[vmem] * 11 + [smem] * 4,
        out_specs=(pl.BlockSpec(memory_space=pl.ANY),) * 4 + (vmem,),
        scratch_shapes=[
            pltpu.VMEM(shape[1:], jnp.float32),
            pltpu.VMEM((4,) + shape, jnp.float32),
            pltpu.SemaphoreType.DMA((4, depth)),
        ],
        compiler_params=pltpu.CompilerParams(vmem_limit_bytes=50 * 1024 * 1024),
        cost_estimate=pl.CostEstimate(
            flops=200 * cells, bytes_accessed=4 * cells * 40, transcendentals=0
        ),
    )(e_forward, h_forward, p_forward, j_forward, e_adjoint, h_adjoint, p_adjoint, j_adjoint,
      arrived, upper, below, source_cell, monitor_cell, source_amp, slab_start)


def body(
    e_forward,
    h_forward,
    p_forward,
    j_forward,
    e_adjoint,
    h_adjoint,
    p_adjoint,
    j_adjoint,
    design,
    source_amp,
    source_cell,
    monitor_cell,
    slab_start,
    radius,
):
    count = lax.axis_size("gx")
    index = lax.axis_index("gx")
    depth, width_x, width_y = (e_forward.shape[1], e_forward.shape[2], e_forward.shape[3])
    start = slab_start[0]
    wx = band_matrix(width_x, radius[0])
    wy = band_matrix(width_y, radius[0])
    upper = passed_along(jnp.concatenate([e_forward[0:2, 0], e_adjoint[0:2, 0]], 0), "gx", -1)
    below = passed_along(
        jnp.concatenate(
            [h_forward[0:2, -1], e_forward[:, -1], h_adjoint[0:2, -1], e_adjoint[:, -1]], 0
        ),
        "gx",
        1,
    )
    owned = smooth(wx, wy, design)
    slots = jnp.broadcast_to(owned, (count,) + owned.shape[1:])
    arrived = lax.all_to_all(slots, "gx", split_axis=0, concat_axis=0, tiled=True)
    ef, hf, ea, ha, returned = fields(
        e_forward, h_forward, p_forward, j_forward, e_adjoint, h_adjoint, p_adjoint, j_adjoint,
        arrived, upper, below, source_cell, monitor_cell, source_amp, slab_start,
    )
    arrived_back = lax.all_to_all(returned, "gx", split_axis=0, concat_axis=0, tiled=True)
    inner = jnp.einsum("ax,jab->xb", wx, arrived_back, precision=HIGH)
    design_grad = jnp.einsum("xb,by->xy", inner, wy, precision=HIGH)[None]
    return (ef, hf, ea, ha, design_grad)


def solution(mesh):
    return jax.shard_map(
        body,
        mesh=mesh,
        in_specs=(
            P(None, ("grp", "gx"), None, None),
            P(None, ("grp", "gx"), None, None),
            P(None, ("grp", "gx"), None, None),
            P(None, ("grp", "gx"), None, None),
            P(None, ("grp", "gx"), None, None),
            P(None, ("grp", "gx"), None, None),
            P(None, ("grp", "gx"), None, None),
            P(None, ("grp", "gx"), None, None),
            P(("grp", "gx"), None, None),
            P("grp", None),
            P("grp"),
            P("grp"),
            P("grp"),
            P("grp"),
        ),
        out_specs=(
            P(None, ("grp", "gx"), None, None),
            P(None, ("grp", "gx"), None, None),
            P(None, ("grp", "gx"), None, None),
            P(None, ("grp", "gx"), None, None),
            P(("grp", "gx"), None, None),
        ),
        check_vma=False,
    )
```

```python
import functools

import jax
import jax.numpy as jnp
from jax import lax
from jax.experimental import pallas as pl
from jax.experimental.pallas import tpu as pltpu
from jax.sharding import PartitionSpec as P

DT = 0.5
EPS_RANGE = 10.0
STRENGTH_BASE = 0.5
STRENGTH_RANGE = 3.0
DAMPING = 0.2
GAIN_FIELD = 0.25
HIGH = lax.Precision.HIGHEST
KEEP = 1.0 - DAMPING * DT / 2.0
LOSS = 1.0 + DAMPING * DT / 2.0
SHRINK = 1.0 / LOSS


def passed_along(block, axis, distance):
    devices = range(lax.axis_size(axis))
    route = [(i - distance, i) for i in devices if i - distance in devices]
    return lax.ppermute(block, axis, route)


def band_matrix(count, radius):
    rows = jnp.arange(count, dtype=jnp.int32)
    dist = jnp.abs(rows[:, None] - rows[None, :])
    weights = jnp.maximum(radius + 1 - dist, 0).astype(jnp.float32)
    return weights / jnp.sum(weights, axis=1, keepdims=True)


def smooth(wx, wy, planes):
    inner = jnp.einsum("ax,zxy->zay", wx, planes, precision=HIGH)
    return jnp.einsum("zay,by->zab", inner, wy, precision=HIGH)


def smooth_adjoint(wx, wy, planes):
    inner = jnp.einsum("ax,zab->zxb", wx, planes, precision=HIGH)
    return jnp.einsum("zxb,by->zxy", inner, wy, precision=HIGH)


def split_cell(cell, width_x, width_y):
    plane = width_x * width_y
    if plane & (plane - 1) == 0 and width_y & (width_y - 1) == 0:
        zz = lax.shift_right_arithmetic(cell, plane.bit_length() - 1)
        rest = lax.bitwise_and(cell, plane - 1)
        x = lax.shift_right_arithmetic(rest, width_y.bit_length() - 1)
        return zz, x, lax.bitwise_and(rest, width_y - 1)
    zz = cell // plane
    rest = cell - zz * plane
    x = rest // width_y
    return zz, x, rest - x * width_y


def field_kernel(
    ef, hf, pf, jf, ea, ha, pa, ja, arrived, upper, below, src, mon, amp, first,
    ef_oh, hf_oh, ea_oh, ha_oh, ret_o, rho, outs, out_sem,
):
    depth, width_x, width_y = rho.shape
    ef_o, hf_o, ea_o, ha_o = (outs.at[a] for a in range(4))
    targets = (ef_oh, hf_oh, ea_oh, ha_oh)

    def store(a, z):
        return pltpu.make_async_copy(
            outs.at[a, :, pl.ds(z, 1)], targets[a].at[:, pl.ds(z, 1)], out_sem.at[a, z]
        )

    slab = arrived.shape[0]
    index = lax.axis_index("gx")
    start = first[0]
    for z in range(depth):
        p = index * depth + z - start
        inside = (p >= 0) & (p < slab)
        rho[z] = jnp.where(inside, arrived[jnp.clip(p, 0, slab - 1)], 0.0)
    row = lax.broadcasted_iota(jnp.int32, (width_x, width_y), 0)
    lane = lax.broadcasted_iota(jnp.int32, (width_x, width_y), 1)

    def ahead_y(f):
        return jnp.where(lane == width_y - 1, 0.0, pltpu.roll(f, width_y - 1, 1))

    def ahead_x(f):
        return jnp.where(row == width_x - 1, 0.0, pltpu.roll(f, width_x - 1, 0))

    def behind_y(f):
        return jnp.where(lane == 0, 0.0, pltpu.roll(f, 1, 1))

    def behind_x(f):
        return jnp.where(row == 0, 0.0, pltpu.roll(f, 1, 0))

    def new_h(e, h, z, ex_up, ey_up):
        ex, ey, ez = e[0, z], e[1, z], e[2, z]
        curl_x = ahead_y(ez) - ez - (ey_up - ey)
        curl_y = ex_up - ex - (ahead_x(ez) - ez)
        curl_z = ahead_x(ey) - ey - (ahead_y(ex) - ex)
        return (h[0, z] - DT * curl_x, h[1, z] - DT * curl_y, h[2, z] - DT * curl_z)

    def lower_h(e, base):
        hx, hy, ex, ey, ez = (below[base + i] for i in range(5))
        curl_x = ahead_y(ez) - ez - (e[1, 0] - ey)
        curl_y = e[0, 0] - ex - (ahead_x(ez) - ez)
        keep = index > 0
        return (
            jnp.where(keep, hx - DT * curl_x, 0.0),
            jnp.where(keep, hy - DT * curl_y, 0.0),
        )

    def new_e(e, p, j, out, z, hn, hn_dn, step, strength):
        hx, hy, hz = hn
        hx_dn, hy_dn = hn_dn
        curl = (
            hz - behind_y(hz) - (hy - hy_dn),
            hx - hx_dn - (hz - behind_x(hz)),
            hy - behind_x(hy) - (hx - behind_y(hx)),
        )
        for c in range(3):
            j_next = (KEEP * j[c, z] + DT * (strength * e[c, z] - p[c, z])) * SHRINK
            out[c, z] = e[c, z] + step * (curl[c] - j_next)

    runs = ((ef, hf, pf, jf, hf_o, ef_o, 0), (ea, ha, pa, ja, ha_o, ea_o, 2))
    for z in range(depth):
        for r, (e, h, p, j, h_out, e_out, up) in enumerate(runs):
            if z + 1 < depth:
                ex_up, ey_up = e[0, z + 1], e[1, z + 1]
            else:
                ex_up, ey_up = upper[up], upper[up + 1]
            hn = new_h(e, h, z, ex_up, ey_up)
            for c in range(3):
                h_out[c, z] = hn[c]
            store(2 * r + 1, z).start()
    prev = [lower_h(ef, 0), lower_h(ea, 5)]
    for z in range(depth):
        density = rho[z]
        step = DT / (1.0 + EPS_RANGE * density)
        strength = STRENGTH_BASE + STRENGTH_RANGE * density
        for r, (e, h, p, j, h_out, e_out, up) in enumerate(runs):
            hn = (h_out[0, z], h_out[1, z], h_out[2, z])
            hn_dn = prev[r] if z == 0 else (h_out[0, z - 1], h_out[1, z - 1])
            new_e(e, p, j, e_out, z, hn, hn_dn, step, strength)

    plane = width_x * width_y
    tile_row = lax.broadcasted_iota(jnp.int32, (8, width_y), 0)
    tile_lane = lax.broadcasted_iota(jnp.int32, (8, width_y), 1)

    def add_at(cell, out, value_of):
        zz, x, y = split_cell(cell, width_x, width_y)
        local = zz - index * depth
        x0 = pl.multiple_of(x - lax.bitwise_and(x, 7), 8)

        @pl.when((local >= 0) & (local < depth))
        def _():
            rows = pl.ds(x0, 8)
            hit = (tile_row == x - x0) & (tile_lane == y)
            step = DT / (1.0 + EPS_RANGE * rho[local, rows, :])
            for c in range(3):
                held = out[c, local, rows, :]
                out[c, local, rows, :] = held + jnp.where(hit, step * value_of(c, local, rows), 0.0)

    for s in range(src.shape[0]):
        add_at(src[s], ef_o, lambda c, local, rows, s=s: amp[s, c])
    for m in range(mon.shape[0]):
        add_at(mon[m], ea_o, lambda c, local, rows: ef[c, local, rows, :])

    for z in range(depth):
        store(0, z).start()
        store(2, z).start()
    for g in range(slab):
        ret_o[g] = jnp.zeros((width_x, width_y), jnp.float32)
    for z in range(depth):
        total = None
        for c in range(3):
            fwd = ef_o[c, z]
            term = ea_o[c, z] * (fwd - ef[c, z] + GAIN_FIELD * fwd)
            total = term if total is None else total + term
        p = index * depth + z - start

        @pl.when((p >= 0) & (p < slab))
        def _():
            ret_o[jnp.clip(p, 0, slab - 1)] = total

    for z in range(depth):
        for a in range(4):
            store(a, z).wait()


def fields(e_forward, h_forward, p_forward, j_forward, e_adjoint, h_adjoint, p_adjoint, j_adjoint,
           arrived, upper, below, source_cell, monitor_cell, source_amp, slab_start):
    shape = e_forward.shape
    depth = shape[1]
    field = jax.ShapeDtypeStruct(shape, jnp.float32)
    vmem = pl.BlockSpec(memory_space=pltpu.VMEM)
    smem = pl.BlockSpec(memory_space=pltpu.SMEM)
    cells = shape[1] * shape[2] * shape[3]
    return pl.pallas_call(
        field_kernel,
        out_shape=(field, field, field, field, jax.ShapeDtypeStruct(arrived.shape, jnp.float32)),
        in_specs=[vmem] * 11 + [smem] * 4,
        out_specs=(pl.BlockSpec(memory_space=pl.ANY),) * 4 + (vmem,),
        scratch_shapes=[
            pltpu.VMEM(shape[1:], jnp.float32),
            pltpu.VMEM((4,) + shape, jnp.float32),
            pltpu.SemaphoreType.DMA((4, depth)),
        ],
        compiler_params=pltpu.CompilerParams(vmem_limit_bytes=50 * 1024 * 1024),
        cost_estimate=pl.CostEstimate(
            flops=200 * cells, bytes_accessed=4 * cells * 40, transcendentals=0
        ),
    )(e_forward, h_forward, p_forward, j_forward, e_adjoint, h_adjoint, p_adjoint, j_adjoint,
      arrived, upper, below, source_cell, monitor_cell, source_amp, slab_start)


def body(
    e_forward,
    h_forward,
    p_forward,
    j_forward,
    e_adjoint,
    h_adjoint,
    p_adjoint,
    j_adjoint,
    design,
    source_amp,
    source_cell,
    monitor_cell,
    slab_start,
    radius,
):
    count = lax.axis_size("gx")
    index = lax.axis_index("gx")
    depth, width_x, width_y = (e_forward.shape[1], e_forward.shape[2], e_forward.shape[3])
    start = slab_start[0]
    wx = band_matrix(width_x, radius[0])
    wy = band_matrix(width_y, radius[0])
    upper = passed_along(jnp.concatenate([e_forward[0:2, 0], e_adjoint[0:2, 0]], 0), "gx", -1)
    below = passed_along(
        jnp.concatenate(
            [h_forward[0:2, -1], e_forward[:, -1], h_adjoint[0:2, -1], e_adjoint[:, -1]], 0
        ),
        "gx",
        1,
    )
    owned = smooth(wx, wy, design)
    slots = jnp.broadcast_to(owned, (count,) + owned.shape[1:])
    arrived = lax.all_to_all(slots, "gx", split_axis=0, concat_axis=0, tiled=True)
    ef, hf, ea, ha, returned = fields(
        e_forward, h_forward, p_forward, j_forward, e_adjoint, h_adjoint, p_adjoint, j_adjoint,
        arrived, upper, below, source_cell, monitor_cell, source_amp, slab_start,
    )
    arrived_back = lax.all_to_all(returned, "gx", split_axis=0, concat_axis=0, tiled=True)
    inner = jnp.einsum("ax,jab->xb", wx, arrived_back, precision=HIGH)
    design_grad = jnp.einsum("xb,by->xy", inner, wy, precision=HIGH)[None]
    return (ef, hf, ea, ha, design_grad)


def solution(mesh):
    return jax.shard_map(
        body,
        mesh=mesh,
        in_specs=(
            P(None, ("grp", "gx"), None, None),
            P(None, ("grp", "gx"), None, None),
            P(None, ("grp", "gx"), None, None),
            P(None, ("grp", "gx"), None, None),
            P(None, ("grp", "gx"), None, None),
            P(None, ("grp", "gx"), None, None),
            P(None, ("grp", "gx"), None, None),
            P(None, ("grp", "gx"), None, None),
            P(("grp", "gx"), None, None),
            P("grp", None),
            P("grp"),
            P("grp"),
            P("grp"),
            P("grp"),
        ),
        out_specs=(
            P(None, ("grp", "gx"), None, None),
            P(None, ("grp", "gx"), None, None),
            P(None, ("grp", "gx"), None, None),
            P(None, ("grp", "gx"), None, None),
            P(("grp", "gx"), None, None),
        ),
        check_vma=False,
    )
```

```python
import functools

import jax
import jax.numpy as jnp
from jax import lax
from jax.experimental import pallas as pl
from jax.experimental.pallas import tpu as pltpu
from jax.sharding import PartitionSpec as P

DT = 0.5
EPS_RANGE = 10.0
STRENGTH_BASE = 0.5
STRENGTH_RANGE = 3.0
DAMPING = 0.2
GAIN_FIELD = 0.25
HIGH = lax.Precision.HIGHEST
KEEP = 1.0 - DAMPING * DT / 2.0
LOSS = 1.0 + DAMPING * DT / 2.0
SHRINK = 1.0 / LOSS
KEEP_SHRUNK = KEEP / LOSS
DT_SHRUNK = DT / LOSS
AHEAD_GAIN = 1.0 + GAIN_FIELD


def passed_along(block, axis, distance):
    devices = range(lax.axis_size(axis))
    route = [(i - distance, i) for i in devices if i - distance in devices]
    return lax.ppermute(block, axis, route)


def band_matrix(count, radius):
    rows = jnp.arange(count, dtype=jnp.int32)
    dist = jnp.abs(rows[:, None] - rows[None, :])
    weights = jnp.maximum(radius + 1 - dist, 0).astype(jnp.float32)
    return weights / jnp.sum(weights, axis=1, keepdims=True)


def smooth(wx, wy, planes):
    inner = jnp.einsum("ax,zxy->zay", wx, planes, precision=HIGH)
    return jnp.einsum("zay,by->zab", inner, wy, precision=HIGH)


def smooth_adjoint(wx, wy, planes):
    inner = jnp.einsum("ax,zab->zxb", wx, planes, precision=HIGH)
    return jnp.einsum("zxb,by->zxy", inner, wy, precision=HIGH)


def split_cell(cell, width_x, width_y):
    plane = width_x * width_y
    if plane & (plane - 1) == 0 and width_y & (width_y - 1) == 0:
        zz = lax.shift_right_arithmetic(cell, plane.bit_length() - 1)
        rest = lax.bitwise_and(cell, plane - 1)
        x = lax.shift_right_arithmetic(rest, width_y.bit_length() - 1)
        return zz, x, lax.bitwise_and(rest, width_y - 1)
    zz = cell // plane
    rest = cell - zz * plane
    x = rest // width_y
    return zz, x, rest - x * width_y


def field_kernel(
    ef, hf, pf, jf, ea, ha, pa, ja, arrived, upper, below, src, mon, amp, first,
    ef_oh, hf_oh, ea_oh, ha_oh, ret_o, rho, outs, out_sem,
):
    depth, width_x, width_y = rho.shape
    ef_o, hf_o, ea_o, ha_o = (outs.at[a] for a in range(4))
    targets = (ef_oh, hf_oh, ea_oh, ha_oh)

    def store(a, z):
        return pltpu.make_async_copy(
            outs.at[a, :, pl.ds(z, 1)], targets[a].at[:, pl.ds(z, 1)], out_sem.at[a, z]
        )

    slab = arrived.shape[0]
    index = lax.axis_index("gx")
    start = first[0]
    for z in range(depth):
        p = index * depth + z - start
        inside = (p >= 0) & (p < slab)
        rho[z] = jnp.where(inside, arrived[jnp.clip(p, 0, slab - 1)], 0.0)
    row = lax.broadcasted_iota(jnp.int32, (width_x, width_y), 0)
    lane = lax.broadcasted_iota(jnp.int32, (width_x, width_y), 1)

    def ahead_y(f):
        return jnp.where(lane == width_y - 1, 0.0, pltpu.roll(f, width_y - 1, 1))

    def ahead_x(f):
        return jnp.where(row == width_x - 1, 0.0, pltpu.roll(f, width_x - 1, 0))

    def behind_y(f):
        return jnp.where(lane == 0, 0.0, pltpu.roll(f, 1, 1))

    def behind_x(f):
        return jnp.where(row == 0, 0.0, pltpu.roll(f, 1, 0))

    def new_h(e, h, z, ex_up, ey_up):
        ex, ey, ez = e[0, z], e[1, z], e[2, z]
        curl_x = ahead_y(ez) - ez - (ey_up - ey)
        curl_y = ex_up - ex - (ahead_x(ez) - ez)
        curl_z = ahead_x(ey) - ey - (ahead_y(ex) - ex)
        return (h[0, z] - DT * curl_x, h[1, z] - DT * curl_y, h[2, z] - DT * curl_z)

    def lower_h(e, base):
        hx, hy, ex, ey, ez = (below[base + i] for i in range(5))
        curl_x = ahead_y(ez) - ez - (e[1, 0] - ey)
        curl_y = e[0, 0] - ex - (ahead_x(ez) - ez)
        keep = index > 0
        return (
            jnp.where(keep, hx - DT * curl_x, 0.0),
            jnp.where(keep, hy - DT * curl_y, 0.0),
        )

    def new_e(e, p, j, out, z, hn, hn_dn, step, drift):
        hx, hy, hz = hn
        hx_dn, hy_dn = hn_dn
        curl = (
            hz - behind_y(hz) - (hy - hy_dn),
            hx - hx_dn - (hz - behind_x(hz)),
            hy - behind_x(hy) - (hx - behind_y(hx)),
        )
        for c in range(3):
            j_next = KEEP_SHRUNK * j[c, z] + drift * e[c, z] - DT_SHRUNK * p[c, z]
            out[c, z] = e[c, z] + step * (curl[c] - j_next)

    runs = ((ef, hf, pf, jf, hf_o, ef_o, 0), (ea, ha, pa, ja, ha_o, ea_o, 2))
    for z in range(depth):
        for r, (e, h, p, j, h_out, e_out, up) in enumerate(runs):
            if z + 1 < depth:
                ex_up, ey_up = e[0, z + 1], e[1, z + 1]
            else:
                ex_up, ey_up = upper[up], upper[up + 1]
            hn = new_h(e, h, z, ex_up, ey_up)
            for c in range(3):
                h_out[c, z] = hn[c]
            store(2 * r + 1, z).start()
    prev = [lower_h(ef, 0), lower_h(ea, 5)]
    for z in range(depth):
        density = rho[z]
        step = DT / (1.0 + EPS_RANGE * density)
        drift = DT_SHRUNK * (STRENGTH_BASE + STRENGTH_RANGE * density)
        for r, (e, h, p, j, h_out, e_out, up) in enumerate(runs):
            hn = (h_out[0, z], h_out[1, z], h_out[2, z])
            hn_dn = prev[r] if z == 0 else (h_out[0, z - 1], h_out[1, z - 1])
            new_e(e, p, j, e_out, z, hn, hn_dn, step, drift)

    plane = width_x * width_y
    tile_row = lax.broadcasted_iota(jnp.int32, (8, width_y), 0)
    tile_lane = lax.broadcasted_iota(jnp.int32, (8, width_y), 1)

    def add_at(cell, out, value_of):
        zz, x, y = split_cell(cell, width_x, width_y)
        local = zz - index * depth
        x0 = pl.multiple_of(x - lax.bitwise_and(x, 7), 8)

        @pl.when((local >= 0) & (local < depth))
        def _():
            rows = pl.ds(x0, 8)
            hit = (tile_row == x - x0) & (tile_lane == y)
            step = DT / (1.0 + EPS_RANGE * rho[local, rows, :])
            for c in range(3):
                held = out[c, local, rows, :]
                out[c, local, rows, :] = held + jnp.where(hit, step * value_of(c, local, rows), 0.0)

    for s in range(src.shape[0]):
        add_at(src[s], ef_o, lambda c, local, rows, s=s: amp[s, c])
    for m in range(mon.shape[0]):
        add_at(mon[m], ea_o, lambda c, local, rows: ef[c, local, rows, :])

    for z in range(depth):
        store(0, z).start()
        store(2, z).start()
    for g in range(slab):
        ret_o[g] = jnp.zeros((width_x, width_y), jnp.float32)
    for z in range(depth):
        total = None
        for c in range(3):
            fwd = ef_o[c, z]
            term = ea_o[c, z] * (AHEAD_GAIN * fwd - ef[c, z])
            total = term if total is None else total + term
        p = index * depth + z - start

        @pl.when((p >= 0) & (p < slab))
        def _():
            ret_o[jnp.clip(p, 0, slab - 1)] = total

    for z in range(depth):
        for a in range(4):
            store(a, z).wait()


def fields(e_forward, h_forward, p_forward, j_forward, e_adjoint, h_adjoint, p_adjoint, j_adjoint,
           arrived, upper, below, source_cell, monitor_cell, source_amp, slab_start):
    shape = e_forward.shape
    depth = shape[1]
    field = jax.ShapeDtypeStruct(shape, jnp.float32)
    vmem = pl.BlockSpec(memory_space=pltpu.VMEM)
    smem = pl.BlockSpec(memory_space=pltpu.SMEM)
    cells = shape[1] * shape[2] * shape[3]
    return pl.pallas_call(
        field_kernel,
        out_shape=(field, field, field, field, jax.ShapeDtypeStruct(arrived.shape, jnp.float32)),
        in_specs=[vmem] * 11 + [smem] * 4,
        out_specs=(pl.BlockSpec(memory_space=pl.ANY),) * 4 + (vmem,),
        scratch_shapes=[
            pltpu.VMEM(shape[1:], jnp.float32),
            pltpu.VMEM((4,) + shape, jnp.float32),
            pltpu.SemaphoreType.DMA((4, depth)),
        ],
        compiler_params=pltpu.CompilerParams(vmem_limit_bytes=50 * 1024 * 1024),
        cost_estimate=pl.CostEstimate(
            flops=200 * cells, bytes_accessed=4 * cells * 40, transcendentals=0
        ),
    )(e_forward, h_forward, p_forward, j_forward, e_adjoint, h_adjoint, p_adjoint, j_adjoint,
      arrived, upper, below, source_cell, monitor_cell, source_amp, slab_start)


def body(
    e_forward,
    h_forward,
    p_forward,
    j_forward,
    e_adjoint,
    h_adjoint,
    p_adjoint,
    j_adjoint,
    design,
    source_amp,
    source_cell,
    monitor_cell,
    slab_start,
    radius,
):
    count = lax.axis_size("gx")
    index = lax.axis_index("gx")
    depth, width_x, width_y = (e_forward.shape[1], e_forward.shape[2], e_forward.shape[3])
    start = slab_start[0]
    wx = band_matrix(width_x, radius[0])
    wy = band_matrix(width_y, radius[0])
    upper = passed_along(jnp.concatenate([e_forward[0:2, 0], e_adjoint[0:2, 0]], 0), "gx", -1)
    below = passed_along(
        jnp.concatenate(
            [h_forward[0:2, -1], e_forward[:, -1], h_adjoint[0:2, -1], e_adjoint[:, -1]], 0
        ),
        "gx",
        1,
    )
    owned = smooth(wx, wy, design)
    slots = jnp.broadcast_to(owned, (count,) + owned.shape[1:])
    arrived = lax.all_to_all(slots, "gx", split_axis=0, concat_axis=0, tiled=True)
    ef, hf, ea, ha, returned = fields(
        e_forward, h_forward, p_forward, j_forward, e_adjoint, h_adjoint, p_adjoint, j_adjoint,
        arrived, upper, below, source_cell, monitor_cell, source_amp, slab_start,
    )
    arrived_back = lax.all_to_all(returned, "gx", split_axis=0, concat_axis=0, tiled=True)
    inner = jnp.einsum("ax,jab->xb", wx, arrived_back, precision=HIGH)
    design_grad = jnp.einsum("xb,by->xy", inner, wy, precision=HIGH)[None]
    return (ef, hf, ea, ha, design_grad)


def solution(mesh):
    return jax.shard_map(
        body,
        mesh=mesh,
        in_specs=(
            P(None, ("grp", "gx"), None, None),
            P(None, ("grp", "gx"), None, None),
            P(None, ("grp", "gx"), None, None),
            P(None, ("grp", "gx"), None, None),
            P(None, ("grp", "gx"), None, None),
            P(None, ("grp", "gx"), None, None),
            P(None, ("grp", "gx"), None, None),
            P(None, ("grp", "gx"), None, None),
            P(("grp", "gx"), None, None),
            P("grp", None),
            P("grp"),
            P("grp"),
            P("grp"),
            P("grp"),
        ),
        out_specs=(
            P(None, ("grp", "gx"), None, None),
            P(None, ("grp", "gx"), None, None),
            P(None, ("grp", "gx"), None, None),
            P(None, ("grp", "gx"), None, None),
            P(("grp", "gx"), None, None),
        ),
        check_vma=False,
    )
```
